128 devices in a mesh: lat: 8 (over z_hi, y), lon: 16 (over z_lo, x, core).
Axes of the slice: x: 4, y: 4, z: 4 (z_hi: 2, z_lo: 2; z = z_hi * 2 + z_lo), core: 2. Of those that a mesh axis runs over, the one named last changes fastest.
Arguments:
- atmosphere: bfloat16 [128, 1024, 384], P('lat', 'lon'), may hold values from -6 to 6
- ocean_state: bfloat16 [131072, 256], P(('lat', 'lon')), may hold values from -6 to 6
- dilation: int32 [384], replicated, may hold values from 1 to 4, as said below
- conv_taps: float32 [5, 384], replicated, may hold values from -3 to 3
- atmosphere_gain: float32 [384], replicated, may hold values from 0.1 to 1.9
- ocean_gain: float32 [256], replicated, may hold values from 0.1 to 1.9
- inner_weight: bfloat16 [384, 1536], replicated, may hold values from -0.3125 to 0.3125
- outer_weight: bfloat16 [1536, 384], replicated, may hold values from -0.15625 to 0.15625
- flux_weight: bfloat16 [384, 256], replicated, may hold values from -0.3125 to 0.3125
- ocean_inner: bfloat16 [256, 1024], replicated, may hold values from -0.375 to 0.375
- ocean_outer: bfloat16 [1024, 256], replicated, may hold values from -0.1875 to 0.1875
- land_sea: int32 [128, 1024], P('lat', 'lon'), may hold values 0 or 1
- send_cell: int32 [128, 128, 16], P(('lat', 'lon')), may hold values from 0 to 1023
- slot_counts: int32 [128, 128], P(('lat', 'lon')), may hold values from 0 to 16, as said below
- slot_area: float32 [128, 128, 16], P(('lat', 'lon')), may hold values from 0.2 to 1
- recv_cell: int32 [128, 128, 16], P(('lat', 'lon')), may hold values from 0 to 1023
- atmosphere_cot: bfloat16 [128, 1024, 384], P('lat', 'lon'), may hold values from -6 to 6
- ocean_cot: bfloat16 [131072, 256], P(('lat', 'lon')), may hold values from -6 to 6
Outputs:
- grad_atmosphere: bfloat16 [128, 1024, 384], P('lat', 'lon')
- grad_ocean: bfloat16 [131072, 256], P(('lat', 'lon'))
- grad_inner: float32 [384, 1536], replicated
- grad_outer: float32 [1536, 384], replicated
- grad_flux_weight: float32 [384, 256], replicated
- grad_ocean_inner: float32 [256, 1024], replicated
- grad_ocean_outer: float32 [1024, 256], replicated
The draws below stay inside these ranges and needn't reach their ends.
Inputs may be any that keep to these rules, and one draw needn't show every extreme that they name: `dilation`: some channel has rate 4 and some has rate 1. `slot_counts`: some ocean owner receives 16 live slots from every source device.
All inputs are finite; a program needn't handle non-finite values. No bound on the sum of `land_sea` on one device may be relied on, other than what follows from the above.
Results may differ from the reference program's by a relative error of at most 0.0069.
Values may be sent and summed in bfloat16 or wider, within the bound.
No kernel may reach another device: no remote copies, remote signals or barrier semaphores. Data moves between devices by JAX's collectives and lax.ppermute only.
A program may use at most 128 MiB of HBM per device.

```python
import jax
import jax.numpy as jnp
from jax import lax

CA = 384
HA = 1536
CO = 256
HO = 1024
DMAX = 4
CAP = 16
HL = 16
WL = 64
OC_DEV = 1024
NLAT = 128
NLON = 1024
CELLS = 1024
OCN = 131072
N_LAT = 8
N_LON = 16
DEVICES = 128


def draw_dilation(key, part):
    rates = jax.random.randint(key, (CA,), 1, DMAX + 1)
    where_top = jax.random.randint(jax.random.fold_in(key, 7), (), 0, CA)
    rates = rates.at[where_top].set(DMAX)
    rates = rates.at[(where_top + 1) % CA].set(1)
    return rates.astype(jnp.int32)


def draw_slot_counts(key, part):
    first, second, third, fourth = jax.random.split(jax.random.fold_in(key, 11), 4)
    base = jax.random.randint(first, (DEVICES, DEVICES), CAP // 4, 3 * CAP // 4 + 1)
    heavy = jax.random.randint(second, (DEVICES,), 0, 8) == 0
    full_owner = jax.random.randint(third, (), 0, DEVICES)
    high = jax.random.randint(fourth, (DEVICES, DEVICES), CAP // 2, CAP + 1)
    counts = jnp.where(heavy[None, :], high, base)
    counts = jnp.where(jnp.arange(DEVICES)[None, :] == full_owner, CAP, counts)
    return counts.astype(jnp.int32)


def with_ends(array, stream_key, least, high):
    longest = array.shape.index(max(array.shape))
    spots = []
    for shift in (0, 1):
        where = [jax.random.randint(jax.random.fold_in(stream_key, axis), (), 0, length) for axis, length in enumerate(array.shape)]
        where[longest] = (where[longest] + shift) % array.shape[longest]
        spots.append(tuple(where))
    return array.at[spots[0]].set(least).at[spots[1]].set(high)


def block_scale(rng, dims, shards, least, largest):
    level, own = 1.0, jax.random.fold_in(rng, 6)
    for axis_at, parts in shards:
        heights = jnp.exp(jax.random.uniform(jax.random.fold_in(own, axis_at), (parts,), jnp.float32, least / len(shards), largest / len(shards)))
        level = level * jnp.repeat(heights, dims[axis_at] // parts).reshape([-1 if axis == axis_at else 1 for axis in range(len(dims))])
    return level


def noise(rng, dims, scale, reach, cuts=(), held_as=jnp.bfloat16):
    entries = jax.random.normal(rng, dims, jnp.float32) * scale
    if len(cuts) > 0:
        entries = block_scale(rng, dims, cuts, -0.22, 0.18) * entries
    return jnp.clip(entries, min=-reach, max=reach).astype(held_as)


def setup_inputs(seed: int = 0) -> dict:
    keys = jax.random.split(jax.random.key(seed), 19)
    return {
        "atmosphere": noise(keys[0], (NLAT, NLON, CA), 1.0, 6.0, ((0, 8), (1, 16))),
        "ocean_state": noise(keys[1], (OCN, CO), 1.0, 6.0, ((0, 128),)),
        "dilation": draw_dilation(jax.random.fold_in(keys[18], 71), 0),
        "conv_taps": noise(keys[3], (5, CA), 0.5, 3.0, (), jnp.float32),
        "atmosphere_gain": jnp.clip(1.0 + 0.18 * jax.random.normal(keys[4], (CA,), jnp.float32), 0.1, 1.9),
        "ocean_gain": jnp.clip(1.0 + 0.18 * jax.random.normal(keys[5], (CO,), jnp.float32), 0.1, 1.9),
        "inner_weight": noise(keys[6], (CA, HA), CA ** -0.5, 0.3125),
        "outer_weight": noise(keys[7], (HA, CA), HA ** -0.5, 0.15625),
        "flux_weight": noise(keys[8], (CA, CO), CA ** -0.5, 0.3125),
        "ocean_inner": noise(keys[9], (CO, HO), CO ** -0.5, 0.375),
        "ocean_outer": noise(keys[10], (HO, CO), HO ** -0.5, 0.1875),
        "land_sea": with_ends((jax.random.randint(keys[11], (NLAT, NLON), 0, 3) < 2).astype(jnp.int32), jax.random.fold_in(keys[11], 1), 0, 1),
        "send_cell": with_ends(jax.random.randint(keys[12], (DEVICES, DEVICES, CAP), 0, CELLS), jax.random.fold_in(keys[12], 1), 0, CELLS - 1).astype(jnp.int32),
        "slot_counts": draw_slot_counts(jax.random.fold_in(keys[18], 71), 0),
        "slot_area": jnp.clip(0.2 + 0.8 * jax.random.uniform(keys[14], (DEVICES, DEVICES, CAP), jnp.float32) ** block_scale(keys[14], (DEVICES, DEVICES, CAP), ((0, 128),), -0.2, 0.2), 0.2, 1.0),
        "recv_cell": with_ends(jax.random.randint(keys[15], (DEVICES, DEVICES, CAP), 0, OC_DEV), jax.random.fold_in(keys[15], 1), 0, OC_DEV - 1).astype(jnp.int32),
        "atmosphere_cot": noise(keys[16], (NLAT, NLON, CA), 1.0, 6.0, ((0, 8), (1, 16))),
        "ocean_cot": noise(keys[17], (OCN, CO), 1.0, 6.0, ((0, 128),)),
    }


def silu_slope(value):
    sig = jax.nn.sigmoid(value)
    return sig * (1.0 + value * (1.0 - sig))

def extend(field):
    wrapped = jnp.concatenate([field[:, -DMAX:], field, field[:, :DMAX]], axis=1)
    return jnp.pad(wrapped, ((DMAX, DMAX), (0, 0), (0, 0)))

def dilated(extended, conv_taps, dilation, transpose, rows, cols):
    centre = extended[DMAX:DMAX + rows, DMAX:DMAX + cols].astype(jnp.float32)
    result = conv_taps[0] * centre
    for offset in range(1, DMAX + 1):
        select = (dilation == offset).astype(jnp.float32)
        west = extended[DMAX:DMAX + rows, DMAX - offset:DMAX - offset + cols].astype(jnp.float32)
        east = extended[DMAX:DMAX + rows, DMAX + offset:DMAX + offset + cols].astype(jnp.float32)
        south = extended[DMAX - offset:DMAX - offset + rows, DMAX:DMAX + cols].astype(jnp.float32)
        north = extended[DMAX + offset:DMAX + offset + rows, DMAX:DMAX + cols].astype(jnp.float32)
        if transpose:
            west, east, south, north = (east, west, north, south)
        result = result + select * (conv_taps[1] * west + conv_taps[2] * east + conv_taps[3] * south + conv_taps[4] * north)
    return result

def to_blocks(value):
    width = value.shape[-1]
    return value.reshape(N_LAT, HL, N_LON, WL, width).transpose(0, 2, 1, 3, 4).reshape(N_LAT * N_LON, HL * WL, width)

def from_blocks(value):
    width = value.shape[-1]
    return value.reshape(N_LAT, N_LON, HL, WL, width).transpose(0, 2, 1, 3, 4).reshape(N_LAT * HL, N_LON * WL, width)

def reference(atmosphere, ocean_state, dilation, conv_taps, atmosphere_gain, ocean_gain, inner_weight, outer_weight, flux_weight, ocean_inner, ocean_outer, land_sea, send_cell, slot_counts, slot_area, recv_cell, atmosphere_cot, ocean_cot):
    devices = N_LAT * N_LON
    conv = dilated(extend(atmosphere), conv_taps, dilation, False, NLAT, NLON)
    conv_blocks = to_blocks(conv)
    mask_blocks = to_blocks(land_sea[:, :, None].astype(jnp.float32))
    cot_blocks = to_blocks(atmosphere_cot)

    def air_forward(block):
        conv_cells, sea_mask = block
        scale_air = lax.rsqrt(lax.optimization_barrier(jnp.mean(conv_cells * conv_cells, axis=-1, keepdims=True)) + 1e-06)
        normed = (conv_cells * scale_air * atmosphere_gain).astype(jnp.bfloat16)
        pre = jnp.dot(normed, inner_weight, preferred_element_type=jnp.float32)
        hidden = jax.nn.silu(pre).astype(jnp.bfloat16)
        air_out = (conv_cells + jnp.dot(hidden, outer_weight, preferred_element_type=jnp.float32)).astype(jnp.bfloat16)
        flux_rows = (sea_mask * jnp.dot(air_out, flux_weight, preferred_element_type=jnp.float32)).astype(jnp.bfloat16)
        return (air_out, flux_rows)
    air_out, flux_rows = lax.map(air_forward, (conv_blocks, mask_blocks))
    live = (jnp.arange(CAP)[None, None, :] < slot_counts[:, :, None]).astype(jnp.float32)
    slot_scale = slot_area * live
    picked = jnp.take_along_axis(flux_rows, send_cell.reshape(devices, devices * CAP)[:, :, None], axis=1)
    slot_value = (picked.reshape(devices, devices, CAP, CO).astype(jnp.float32) * slot_scale[..., None]).astype(jnp.bfloat16)
    incoming = slot_value.transpose(1, 0, 2, 3)
    sea_blocks = ocean_state.reshape(devices, OC_DEV, CO)
    sea_cots = ocean_cot.reshape(devices, OC_DEV, CO)

    def sea_step(block):
        state, arrived, cells, cot = block
        coupled = jnp.zeros((OC_DEV, CO), jnp.float32).at[cells.reshape(-1)].add(arrived.reshape(-1, CO).astype(jnp.float32))
        sea_in = state.astype(jnp.float32) + coupled
        scale_sea = lax.rsqrt(lax.optimization_barrier(jnp.mean(sea_in * sea_in, axis=-1, keepdims=True)) + 1e-06)
        sea_normed = (sea_in * scale_sea * ocean_gain).astype(jnp.bfloat16)
        sea_pre = jnp.dot(sea_normed, ocean_inner, preferred_element_type=jnp.float32)
        sea_hidden = jax.nn.silu(sea_pre).astype(jnp.bfloat16)
        sea_vdown = jnp.dot(sea_hidden.T, cot, preferred_element_type=jnp.float32)
        sea_ghid = jnp.dot(cot, ocean_outer.T, preferred_element_type=jnp.float32)
        sea_gpre = (sea_ghid * silu_slope(sea_pre)).astype(jnp.bfloat16)
        sea_vup = jnp.dot(sea_normed.T, sea_gpre, preferred_element_type=jnp.float32)
        sea_gnorm = jnp.dot(sea_gpre, ocean_inner.T, preferred_element_type=jnp.float32)
        inner_mean = lax.optimization_barrier(jnp.mean(sea_in * ocean_gain * sea_gnorm, axis=-1, keepdims=True))
        sea_grad = cot.astype(jnp.float32) + scale_sea * ocean_gain * sea_gnorm - sea_in * scale_sea ** 3 * inner_mean
        slot_return = sea_grad[cells.reshape(-1)].astype(jnp.bfloat16).reshape(devices, CAP, CO)
        return (sea_grad.astype(jnp.bfloat16), slot_return, sea_vup, sea_vdown)
    grad_ocean, slot_return, sea_vup, sea_vdown = lax.map(sea_step, (sea_blocks, incoming, recv_cell, sea_cots))
    returned = slot_return.transpose(1, 0, 2, 3)

    def air_backward(block):
        conv_cells, sea_mask, air_rows, back, cells, scale_rows, cot = block
        flux_grad = jnp.zeros((HL * WL, CO), jnp.float32).at[cells.reshape(-1)].add((back.astype(jnp.float32) * scale_rows[..., None]).reshape(-1, CO))
        flux_masked = (sea_mask * flux_grad).astype(jnp.bfloat16)
        flux_wsum = jnp.dot(air_rows.T, flux_masked, preferred_element_type=jnp.float32)
        air_grad = cot.astype(jnp.float32) + jnp.dot(flux_masked, flux_weight.T, preferred_element_type=jnp.float32)
        air_gradb = air_grad.astype(jnp.bfloat16)
        scale_air = lax.rsqrt(lax.optimization_barrier(jnp.mean(conv_cells * conv_cells, axis=-1, keepdims=True)) + 1e-06)
        normed = (conv_cells * scale_air * atmosphere_gain).astype(jnp.bfloat16)
        pre = jnp.dot(normed, inner_weight, preferred_element_type=jnp.float32)
        hidden = jax.nn.silu(pre).astype(jnp.bfloat16)
        outer_sum = jnp.dot(hidden.T, air_gradb, preferred_element_type=jnp.float32)
        hid_grad = jnp.dot(air_gradb, outer_weight.T, preferred_element_type=jnp.float32)
        pre_grad = (hid_grad * silu_slope(pre)).astype(jnp.bfloat16)
        inner_sum = jnp.dot(normed.T, pre_grad, preferred_element_type=jnp.float32)
        norm_grad = jnp.dot(pre_grad, inner_weight.T, preferred_element_type=jnp.float32)
        inner_mean = lax.optimization_barrier(jnp.mean(conv_cells * atmosphere_gain * norm_grad, axis=-1, keepdims=True))
        conv_grad = (air_grad + scale_air * atmosphere_gain * norm_grad - conv_cells * scale_air ** 3 * inner_mean).astype(jnp.bfloat16)
        return (conv_grad, inner_sum, outer_sum, flux_wsum)
    conv_grad, inner_sum, outer_sum, flux_wsum = lax.map(air_backward, (conv_blocks, mask_blocks, air_out, returned, send_cell, slot_scale, cot_blocks))
    conv_grad = from_blocks(conv_grad)
    grad_atmosphere = dilated(extend(conv_grad), conv_taps, dilation, True, NLAT, NLON).astype(jnp.bfloat16)
    air_factor = float(NLAT * NLON) ** (-0.5)
    sea_factor = float(OCN) ** (-0.5)
    return (grad_atmosphere, grad_ocean.reshape(OCN, CO), lax.optimization_barrier(jnp.sum(inner_sum, axis=0)) * air_factor, lax.optimization_barrier(jnp.sum(outer_sum, axis=0)) * air_factor, lax.optimization_barrier(jnp.sum(flux_wsum, axis=0)) * air_factor, lax.optimization_barrier(jnp.sum(sea_vup, axis=0)) * sea_factor, lax.optimization_barrier(jnp.sum(sea_vdown, axis=0)) * sea_factor)
```

```python
import jax
import jax.numpy as jnp
from jax import lax
from jax.sharding import PartitionSpec as P

DMAX = 4


def with_halo(block, sides, width):
    for axis, dim in sides:
        count = lax.axis_size(axis)
        forward = [(i, i + 1) for i in range(count - 1)]
        forward.append((count - 1, 0))
        backward = [(target, source) for source, target in forward]
        low = lax.ppermute(
            lax.slice_in_dim(block, block.shape[dim] - width, None, axis=dim), axis, forward
        )
        high = lax.ppermute(lax.slice_in_dim(block, 0, width, axis=dim), axis, backward)
        block = jnp.concatenate([low, block, high], axis=dim)
    return block


AXES = ("lat", "lon")
RINGS = ("x", "y", "z")


def device_of(zh, y, zl, x, core):
    return (zh * 4 + y) * 16 + zl * 8 + x * 2 + core


def all_devices():
    for zh in range(2):
        for y in range(4):
            for zl in range(2):
                for x in range(4):
                    for core in range(2):
                        yield zh, y, zl, x, core


def core_pairs():
    return [(device_of(zh, y, zl, x, c), device_of(zh, y, zl, x, 1 - c)) for zh, y, zl, x, c in all_devices()]


def ring_pairs(ring, shift):
    pairs = []
    for zh, y, zl, x, c in all_devices():
        tx, ty, tz = x, y, zh * 2 + zl
        if ring == "x":
            tx = (x + shift) % 4
        elif ring == "y":
            ty = (y + shift) % 4
        else:
            tz = (tz + shift) % 4
        pairs.append((device_of(zh, y, zl, x, c), device_of(tz // 2, ty, tz % 2, tx, c)))
    return pairs


def ring_positions():
    lat = lax.axis_index("lat")
    lon = lax.axis_index("lon")
    return {"x": (lon // 2) % 4, "y": lat % 4, "z": (lat // 4) * 2 + lon // 8}, lon % 2


def place(stack, own_at):
    gathered = jnp.zeros_like(stack)
    for s in range(stack.shape[0]):
        gathered = lax.dynamic_update_index_in_dim(gathered, stack[s], (own_at - s) % stack.shape[0], 0)
    return gathered


def tree_allreduce(parts):
    flat = jnp.concatenate([p.reshape(-1) for p in parts])
    total = flat.shape[0]
    unit = 2 * 3 * 64 * 1024
    padded = -(-total // unit) * unit
    block = padded // (2 * 3 * 64)
    data = jnp.pad(flat, (0, padded - total)).reshape(2, 3, 4, 4, 4, block // 128, 128)
    pos, core = ring_positions()
    mine = lax.dynamic_index_in_dim(data, core, 0, keepdims=False)
    other = lax.dynamic_index_in_dim(data, 1 - core, 0, keepdims=False)
    summed = mine + lax.ppermute(other, AXES, core_pairs())
    owned = []
    for colour in range(3):
        chunk = summed[colour]
        for stage in range(3):
            ring = RINGS[(colour + stage) % 3]
            p = pos[ring]
            acc = lax.dynamic_index_in_dim(chunk, p, 0, keepdims=False)
            for s in range(1, 4):
                piece = lax.dynamic_index_in_dim(chunk, (p + s) % 4, 0, keepdims=False)
                acc = acc + lax.ppermute(piece, AXES, ring_pairs(ring, s))
            chunk = acc
        for stage in reversed(range(3)):
            ring = RINGS[(colour + stage) % 3]
            got = [chunk] + [lax.ppermute(chunk, AXES, ring_pairs(ring, s)) for s in range(1, 4)]
            chunk = place(jnp.stack(got), pos[ring])
        owned.append(chunk)
    owned = jnp.stack(owned)
    both = place(jnp.stack([owned, lax.ppermute(owned, AXES, core_pairs())]), core)
    flat = both.reshape(-1)[:total]
    out, at = [], 0
    for p in parts:
        out.append(flat[at : at + p.size].reshape(p.shape))
        at += p.size
    return out


def silu_slope(value):
    sig = jax.nn.sigmoid(value)
    return sig * (1.0 + value * (1.0 - sig))


def dilated(extended, conv_taps, dilation, transpose, rows, cols):
    centre = extended[DMAX : DMAX + rows, DMAX : DMAX + cols].astype(jnp.float32)
    result = conv_taps[0] * centre
    for offset in range(1, DMAX + 1):
        select = (dilation == offset).astype(jnp.float32)
        west = extended[DMAX : DMAX + rows, DMAX - offset : DMAX - offset + cols].astype(
            jnp.float32
        )
        east = extended[DMAX : DMAX + rows, DMAX + offset : DMAX + offset + cols].astype(
            jnp.float32
        )
        south = extended[DMAX - offset : DMAX - offset + rows, DMAX : DMAX + cols].astype(
            jnp.float32
        )
        north = extended[DMAX + offset : DMAX + offset + rows, DMAX : DMAX + cols].astype(
            jnp.float32
        )
        if transpose:
            west, east, south, north = (east, west, north, south)
        result = result + select * (
            conv_taps[1] * west + conv_taps[2] * east + conv_taps[3] * south + conv_taps[4] * north
        )
    return result


def polar_rows(extended, rows):
    band_rows = lax.axis_index("lat") * rows + jnp.arange(-DMAX, rows + DMAX)
    inside = (band_rows >= 0) & (band_rows < lax.axis_size("lat") * rows)
    return extended * inside[:, None, None].astype(extended.dtype)


def local(
    atmosphere,
    ocean_state,
    dilation,
    conv_taps,
    atmosphere_gain,
    ocean_gain,
    inner_weight,
    outer_weight,
    flux_weight,
    ocean_inner,
    ocean_outer,
    land_sea,
    send_cell,
    slot_counts,
    slot_area,
    recv_cell,
    atmosphere_cot,
    ocean_cot,
):
    rows, cols, channels = atmosphere.shape
    cells = rows * cols
    lat_count = lax.axis_size("lat")
    lon_count = lax.axis_size("lon")
    devices = lat_count * lon_count
    slots = send_cell.shape[2]
    sea_width = flux_weight.shape[1]
    sea_cells = ocean_state.shape[0]
    air_factor = float(cells * devices) ** (-0.5)
    sea_factor = float(sea_cells * devices) ** (-0.5)
    extended = polar_rows(with_halo(atmosphere, (("lat", 0), ("lon", 1)), DMAX), rows)
    conv_cells = dilated(extended, conv_taps, dilation, False, rows, cols).reshape(cells, channels)
    scale_air = lax.rsqrt(jnp.mean(conv_cells * conv_cells, axis=-1, keepdims=True) + 1e-06)
    normed = (conv_cells * scale_air * atmosphere_gain).astype(jnp.bfloat16)
    pre = jnp.dot(normed, inner_weight, preferred_element_type=jnp.float32)
    hidden = jax.nn.silu(pre).astype(jnp.bfloat16)
    air_out = (
        conv_cells + jnp.dot(hidden, outer_weight, preferred_element_type=jnp.float32)
    ).astype(jnp.bfloat16)
    sea_mask = land_sea.reshape(cells, 1).astype(jnp.float32)
    flux_rows = (
        sea_mask * jnp.dot(air_out, flux_weight, preferred_element_type=jnp.float32)
    ).astype(jnp.bfloat16)
    live_slots = (jnp.arange(slots)[None, :] < slot_counts[0][:, None]).astype(jnp.float32)
    slot_scale = (slot_area[0] * live_slots)[..., None]
    outgoing = (flux_rows[send_cell[0]].astype(jnp.float32) * slot_scale).astype(jnp.bfloat16)
    arrived = lax.all_to_all(outgoing, ("lat", "lon"), split_axis=0, concat_axis=0, tiled=True)
    coupled = (
        jnp.zeros((sea_cells, sea_width), jnp.float32)
        .at[recv_cell[0].reshape(-1)]
        .add(arrived.reshape(-1, sea_width).astype(jnp.float32))
    )
    sea_in = ocean_state.astype(jnp.float32) + coupled
    scale_sea = lax.rsqrt(jnp.mean(sea_in * sea_in, axis=-1, keepdims=True) + 1e-06)
    sea_normed = (sea_in * scale_sea * ocean_gain).astype(jnp.bfloat16)
    sea_pre = jnp.dot(sea_normed, ocean_inner, preferred_element_type=jnp.float32)
    sea_hidden = jax.nn.silu(sea_pre).astype(jnp.bfloat16)
    sea_vdown = jnp.dot(sea_hidden.T, ocean_cot, preferred_element_type=jnp.float32)
    sea_ghid = jnp.dot(ocean_cot, ocean_outer.T, preferred_element_type=jnp.float32)
    sea_gpre = (sea_ghid * silu_slope(sea_pre)).astype(jnp.bfloat16)
    sea_vup = jnp.dot(sea_normed.T, sea_gpre, preferred_element_type=jnp.float32)
    sea_gnorm = jnp.dot(sea_gpre, ocean_inner.T, preferred_element_type=jnp.float32)
    sea_mean = jnp.mean(sea_in * ocean_gain * sea_gnorm, axis=-1, keepdims=True)
    sea_grad = (
        ocean_cot.astype(jnp.float32)
        + scale_sea * ocean_gain * sea_gnorm
        - sea_in * scale_sea**3 * sea_mean
    )
    grad_ocean = sea_grad.astype(jnp.bfloat16)
    slot_return = sea_grad[recv_cell[0]].astype(jnp.bfloat16)
    returned = lax.all_to_all(slot_return, ("lat", "lon"), split_axis=0, concat_axis=0, tiled=True)
    flux_grad = (
        jnp.zeros((cells, sea_width), jnp.float32)
        .at[send_cell[0].reshape(-1)]
        .add((returned.astype(jnp.float32) * slot_scale).reshape(-1, sea_width))
    )
    flux_masked = (sea_mask * flux_grad).astype(jnp.bfloat16)
    flux_wsum = jnp.dot(air_out.T, flux_masked, preferred_element_type=jnp.float32)
    air_grad = atmosphere_cot.reshape(cells, channels).astype(jnp.float32) + jnp.dot(
        flux_masked, flux_weight.T, preferred_element_type=jnp.float32
    )
    air_gradb = air_grad.astype(jnp.bfloat16)
    outer_sum = jnp.dot(hidden.T, air_gradb, preferred_element_type=jnp.float32)
    hid_grad = jnp.dot(air_gradb, outer_weight.T, preferred_element_type=jnp.float32)
    pre_grad = (hid_grad * silu_slope(pre)).astype(jnp.bfloat16)
    inner_sum = jnp.dot(normed.T, pre_grad, preferred_element_type=jnp.float32)
    norm_grad = jnp.dot(pre_grad, inner_weight.T, preferred_element_type=jnp.float32)
    air_mean = jnp.mean(conv_cells * atmosphere_gain * norm_grad, axis=-1, keepdims=True)
    conv_grad = (
        air_grad + scale_air * atmosphere_gain * norm_grad - conv_cells * scale_air**3 * air_mean
    ).astype(jnp.bfloat16)
    grad_extended = polar_rows(
        with_halo(conv_grad.reshape(rows, cols, channels), (("lat", 0), ("lon", 1)), DMAX), rows
    )
    grad_atmosphere = dilated(grad_extended, conv_taps, dilation, True, rows, cols).astype(
        jnp.bfloat16
    )
    summed = tree_allreduce((inner_sum, outer_sum, flux_wsum, sea_vup, sea_vdown))
    return (
        grad_atmosphere,
        grad_ocean,
        summed[0] * air_factor,
        summed[1] * air_factor,
        summed[2] * air_factor,
        summed[3] * sea_factor,
        summed[4] * sea_factor,
    )


def solution(mesh):
    in_specs = (
        P("lat", "lon", None),
        P(("lat", "lon"), None),
        P(),
        P(),
        P(),
        P(),
        P(),
        P(),
        P(),
        P(),
        P(),
        P("lat", "lon"),
        P(("lat", "lon"), None, None),
        P(("lat", "lon"), None),
        P(("lat", "lon"), None, None),
        P(("lat", "lon"), None, None),
        P("lat", "lon", None),
        P(("lat", "lon"), None),
    )
    out_specs = (P("lat", "lon", None), P(("lat", "lon"), None), P(), P(), P(), P(), P())
    return jax.shard_map(local, mesh=mesh, in_specs=in_specs, out_specs=out_specs, check_vma=False)
```

```python
import jax
import jax.numpy as jnp
from jax import lax
from jax.sharding import PartitionSpec as P

DMAX = 4


def with_halo(block, sides, width):
    (lat_axis, lat_dim), (lon_axis, lon_dim) = sides
    pieces = []
    for axis, dim in sides:
        count = lax.axis_size(axis)
        forward = [(i, i + 1) for i in range(count - 1)]
        forward.append((count - 1, 0))
        backward = [(target, source) for source, target in forward]
        low = lax.ppermute(
            lax.slice_in_dim(block, block.shape[dim] - width, None, axis=dim), axis, forward
        )
        high = lax.ppermute(lax.slice_in_dim(block, 0, width, axis=dim), axis, backward)
        pieces.append((low, high))
    (south, north), (west, east) = pieces
    rows = jnp.concatenate([south, block, north], axis=lat_dim)
    pad = [(0, 0)] * block.ndim
    pad[lat_dim] = (width, width)
    west = jnp.pad(west, pad)
    east = jnp.pad(east, pad)
    return jnp.concatenate([west, rows, east], axis=lon_dim)


def one_hot(index, size):
    return (index.reshape(-1, 1) == jnp.arange(size)[None, :]).astype(jnp.bfloat16)


def gather_rows(hot, values):
    return jnp.dot(hot, values, preferred_element_type=jnp.float32)


def scatter_rows(hot, values):
    return lax.dot_general(
        hot, values, (((0,), (0,)), ((), ())), preferred_element_type=jnp.float32
    )


def silu_slope(value):
    sig = jax.nn.sigmoid(value)
    return sig * (1.0 + value * (1.0 - sig))


def dilated(extended, conv_taps, dilation, transpose, rows, cols):
    centre = extended[DMAX : DMAX + rows, DMAX : DMAX + cols].astype(jnp.float32)
    result = conv_taps[0] * centre
    for offset in range(1, DMAX + 1):
        select = (dilation == offset).astype(jnp.float32)
        west = extended[DMAX : DMAX + rows, DMAX - offset : DMAX - offset + cols].astype(
            jnp.float32
        )
        east = extended[DMAX : DMAX + rows, DMAX + offset : DMAX + offset + cols].astype(
            jnp.float32
        )
        south = extended[DMAX - offset : DMAX - offset + rows, DMAX : DMAX + cols].astype(
            jnp.float32
        )
        north = extended[DMAX + offset : DMAX + offset + rows, DMAX : DMAX + cols].astype(
            jnp.float32
        )
        if transpose:
            west, east, south, north = (east, west, north, south)
        result = result + select * (
            conv_taps[1] * west + conv_taps[2] * east + conv_taps[3] * south + conv_taps[4] * north
        )
    return result


def polar_rows(extended, rows):
    band_rows = lax.axis_index("lat") * rows + jnp.arange(-DMAX, rows + DMAX)
    inside = (band_rows >= 0) & (band_rows < lax.axis_size("lat") * rows)
    return extended * inside[:, None, None].astype(extended.dtype)


def local(
    atmosphere,
    ocean_state,
    dilation,
    conv_taps,
    atmosphere_gain,
    ocean_gain,
    inner_weight,
    outer_weight,
    flux_weight,
    ocean_inner,
    ocean_outer,
    land_sea,
    send_cell,
    slot_counts,
    slot_area,
    recv_cell,
    atmosphere_cot,
    ocean_cot,
):
    rows, cols, channels = atmosphere.shape
    cells = rows * cols
    lat_count = lax.axis_size("lat")
    lon_count = lax.axis_size("lon")
    devices = lat_count * lon_count
    slots = send_cell.shape[2]
    sea_width = flux_weight.shape[1]
    sea_cells = ocean_state.shape[0]
    air_factor = float(cells * devices) ** (-0.5)
    sea_factor = float(sea_cells * devices) ** (-0.5)
    extended = polar_rows(with_halo(atmosphere, (("lat", 0), ("lon", 1)), DMAX), rows)
    conv_cells = dilated(extended, conv_taps, dilation, False, rows, cols).reshape(cells, channels)
    scale_air = lax.rsqrt(jnp.mean(conv_cells * conv_cells, axis=-1, keepdims=True) + 1e-06)
    normed = (conv_cells * scale_air * atmosphere_gain).astype(jnp.bfloat16)
    pre = jnp.dot(normed, inner_weight, preferred_element_type=jnp.float32)
    hidden = jax.nn.silu(pre).astype(jnp.bfloat16)
    air_out = (
        conv_cells + jnp.dot(hidden, outer_weight, preferred_element_type=jnp.float32)
    ).astype(jnp.bfloat16)
    sea_mask = land_sea.reshape(cells, 1).astype(jnp.float32)
    flux_rows = (
        sea_mask * jnp.dot(air_out, flux_weight, preferred_element_type=jnp.float32)
    ).astype(jnp.bfloat16)
    live_slots = (jnp.arange(slots)[None, :] < slot_counts[0][:, None]).astype(jnp.float32)
    slot_scale = (slot_area[0] * live_slots)[..., None]
    send_hot = one_hot(send_cell[0], cells)
    recv_hot = one_hot(recv_cell[0], sea_cells)
    picked = gather_rows(send_hot, flux_rows).reshape(devices, slots, sea_width)
    outgoing = (picked * slot_scale).astype(jnp.bfloat16)
    arrived = lax.all_to_all(outgoing, ("lat", "lon"), split_axis=0, concat_axis=0, tiled=True)
    coupled = scatter_rows(recv_hot, arrived.reshape(-1, sea_width))
    sea_in = ocean_state.astype(jnp.float32) + coupled
    scale_sea = lax.rsqrt(jnp.mean(sea_in * sea_in, axis=-1, keepdims=True) + 1e-06)
    sea_normed = (sea_in * scale_sea * ocean_gain).astype(jnp.bfloat16)
    sea_pre = jnp.dot(sea_normed, ocean_inner, preferred_element_type=jnp.float32)
    sea_hidden = jax.nn.silu(sea_pre).astype(jnp.bfloat16)
    sea_vdown = jnp.dot(sea_hidden.T, ocean_cot, preferred_element_type=jnp.float32)
    sea_ghid = jnp.dot(ocean_cot, ocean_outer.T, preferred_element_type=jnp.float32)
    sea_gpre = (sea_ghid * silu_slope(sea_pre)).astype(jnp.bfloat16)
    sea_vup = jnp.dot(sea_normed.T, sea_gpre, preferred_element_type=jnp.float32)
    sea_gnorm = jnp.dot(sea_gpre, ocean_inner.T, preferred_element_type=jnp.float32)
    sea_mean = jnp.mean(sea_in * ocean_gain * sea_gnorm, axis=-1, keepdims=True)
    sea_grad = (
        ocean_cot.astype(jnp.float32)
        + scale_sea * ocean_gain * sea_gnorm
        - sea_in * scale_sea**3 * sea_mean
    )
    grad_ocean = sea_grad.astype(jnp.bfloat16)
    slot_return = (
        gather_rows(recv_hot, grad_ocean).astype(jnp.bfloat16).reshape(devices, slots, sea_width)
    )
    returned = lax.all_to_all(slot_return, ("lat", "lon"), split_axis=0, concat_axis=0, tiled=True)
    addends = (returned.astype(jnp.float32) * slot_scale).reshape(-1, sea_width)
    addends_hi = addends.astype(jnp.bfloat16)
    addends_lo = (addends - addends_hi.astype(jnp.float32)).astype(jnp.bfloat16)
    flux_grad = scatter_rows(send_hot, addends_hi) + scatter_rows(send_hot, addends_lo)
    flux_masked = (sea_mask * flux_grad).astype(jnp.bfloat16)
    flux_wsum = jnp.dot(air_out.T, flux_masked, preferred_element_type=jnp.float32)
    air_grad = atmosphere_cot.reshape(cells, channels).astype(jnp.float32) + jnp.dot(
        flux_masked, flux_weight.T, preferred_element_type=jnp.float32
    )
    air_gradb = air_grad.astype(jnp.bfloat16)
    outer_sum = jnp.dot(hidden.T, air_gradb, preferred_element_type=jnp.float32)
    hid_grad = jnp.dot(air_gradb, outer_weight.T, preferred_element_type=jnp.float32)
    pre_grad = (hid_grad * silu_slope(pre)).astype(jnp.bfloat16)
    inner_sum = jnp.dot(normed.T, pre_grad, preferred_element_type=jnp.float32)
    norm_grad = jnp.dot(pre_grad, inner_weight.T, preferred_element_type=jnp.float32)
    air_mean = jnp.mean(conv_cells * atmosphere_gain * norm_grad, axis=-1, keepdims=True)
    conv_grad = (
        air_grad + scale_air * atmosphere_gain * norm_grad - conv_cells * scale_air**3 * air_mean
    ).astype(jnp.bfloat16)
    grad_extended = polar_rows(
        with_halo(conv_grad.reshape(rows, cols, channels), (("lat", 0), ("lon", 1)), DMAX), rows
    )
    grad_atmosphere = dilated(grad_extended, conv_taps, dilation, True, rows, cols).astype(
        jnp.bfloat16
    )
    summed = lax.psum(
        (
            inner_sum * air_factor,
            outer_sum * air_factor,
            flux_wsum * air_factor,
            sea_vup * sea_factor,
            sea_vdown * sea_factor,
        ),
        ("lat", "lon"),
    )
    return (grad_atmosphere, grad_ocean) + tuple(summed)


def solution(mesh):
    in_specs = (
        P("lat", "lon", None),
        P(("lat", "lon"), None),
        P(),
        P(),
        P(),
        P(),
        P(),
        P(),
        P(),
        P(),
        P(),
        P("lat", "lon"),
        P(("lat", "lon"), None, None),
        P(("lat", "lon"), None),
        P(("lat", "lon"), None, None),
        P(("lat", "lon"), None, None),
        P("lat", "lon", None),
        P(("lat", "lon"), None),
    )
    out_specs = (P("lat", "lon", None), P(("lat", "lon"), None), P(), P(), P(), P(), P())
    return jax.shard_map(local, mesh=mesh, in_specs=in_specs, out_specs=out_specs, check_vma=False)
```

```python
import jax
import jax.numpy as jnp
from jax import lax
from jax.sharding import PartitionSpec as P

DMAX = 4


def with_halo(block, sides, width):
    (lat_axis, lat_dim), (lon_axis, lon_dim) = sides
    pieces = []
    for axis, dim in sides:
        count = lax.axis_size(axis)
        forward = [(i, i + 1) for i in range(count - 1)]
        forward.append((count - 1, 0))
        backward = [(target, source) for source, target in forward]
        low = lax.ppermute(
            lax.slice_in_dim(block, block.shape[dim] - width, None, axis=dim), axis, forward
        )
        high = lax.ppermute(lax.slice_in_dim(block, 0, width, axis=dim), axis, backward)
        pieces.append((low, high))
    (south, north), (west, east) = pieces
    rows = jnp.concatenate([south, block, north], axis=lat_dim)
    pad = [(0, 0)] * block.ndim
    pad[lat_dim] = (width, width)
    west = jnp.pad(west, pad)
    east = jnp.pad(east, pad)
    return jnp.concatenate([west, rows, east], axis=lon_dim)


def one_hot(index, size):
    return (index.reshape(-1, 1) == jnp.arange(size)[None, :]).astype(jnp.bfloat16)


def gather_rows(hot, values):
    return jnp.dot(hot, values, preferred_element_type=jnp.float32)


def scatter_rows(hot, values):
    return lax.dot_general(
        hot, values, (((0,), (0,)), ((), ())), preferred_element_type=jnp.float32
    )


def silu_slope(value):
    sig = jax.nn.sigmoid(value)
    return sig * (1.0 + value * (1.0 - sig))


def dilated(extended, conv_taps, dilation, transpose, rows, cols):
    centre = extended[DMAX : DMAX + rows, DMAX : DMAX + cols].astype(jnp.float32)
    result = conv_taps[0] * centre
    for offset in range(1, DMAX + 1):
        select = (dilation == offset).astype(jnp.float32)
        west = extended[DMAX : DMAX + rows, DMAX - offset : DMAX - offset + cols].astype(
            jnp.float32
        )
        east = extended[DMAX : DMAX + rows, DMAX + offset : DMAX + offset + cols].astype(
            jnp.float32
        )
        south = extended[DMAX - offset : DMAX - offset + rows, DMAX : DMAX + cols].astype(
            jnp.float32
        )
        north = extended[DMAX + offset : DMAX + offset + rows, DMAX : DMAX + cols].astype(
            jnp.float32
        )
        if transpose:
            west, east, south, north = (east, west, north, south)
        result = result + select * (
            conv_taps[1] * west + conv_taps[2] * east + conv_taps[3] * south + conv_taps[4] * north
        )
    return result


def dilated_once(extended, conv_taps, dilation, rows, cols):
    centre = extended[DMAX : DMAX + rows, DMAX : DMAX + cols].astype(jnp.float32)
    sides = []
    for row_at, col_at in ((0, -1), (0, 1), (-1, 0), (1, 0)):
        picked = None
        for offset in range(DMAX, 0, -1):
            r0 = DMAX + row_at * offset
            c0 = DMAX + col_at * offset
            window = extended[r0 : r0 + rows, c0 : c0 + cols].astype(jnp.float32)
            picked = window if picked is None else jnp.where(dilation == offset, window, picked)
        sides.append(picked)
    west, east, south, north = sides
    return conv_taps[0] * centre + (
        conv_taps[1] * west + conv_taps[2] * east + conv_taps[3] * south + conv_taps[4] * north
    )


def polar_rows(extended, rows):
    band_rows = lax.axis_index("lat") * rows + jnp.arange(-DMAX, rows + DMAX)
    inside = (band_rows >= 0) & (band_rows < lax.axis_size("lat") * rows)
    return extended * inside[:, None, None].astype(extended.dtype)


def local(
    atmosphere,
    ocean_state,
    dilation,
    conv_taps,
    atmosphere_gain,
    ocean_gain,
    inner_weight,
    outer_weight,
    flux_weight,
    ocean_inner,
    ocean_outer,
    land_sea,
    send_cell,
    slot_counts,
    slot_area,
    recv_cell,
    atmosphere_cot,
    ocean_cot,
):
    rows, cols, channels = atmosphere.shape
    cells = rows * cols
    lat_count = lax.axis_size("lat")
    lon_count = lax.axis_size("lon")
    devices = lat_count * lon_count
    slots = send_cell.shape[2]
    sea_width = flux_weight.shape[1]
    sea_cells = ocean_state.shape[0]
    air_factor = float(cells * devices) ** (-0.5)
    sea_factor = float(sea_cells * devices) ** (-0.5)
    extended = polar_rows(with_halo(atmosphere, (("lat", 0), ("lon", 1)), DMAX), rows)
    conv_cells = lax.optimization_barrier(
        dilated_once(extended, conv_taps, dilation, rows, cols).reshape(cells, channels)
    )
    scale_air = lax.rsqrt(jnp.mean(conv_cells * conv_cells, axis=-1, keepdims=True) + 1e-06)
    normed = (conv_cells * scale_air * atmosphere_gain).astype(jnp.bfloat16)
    pre = jnp.dot(normed, inner_weight, preferred_element_type=jnp.float32)
    hidden = jax.nn.silu(pre).astype(jnp.bfloat16)
    air_out = (
        conv_cells + jnp.dot(hidden, outer_weight, preferred_element_type=jnp.float32)
    ).astype(jnp.bfloat16)
    sea_mask = land_sea.reshape(cells, 1).astype(jnp.float32)
    flux_rows = (
        sea_mask * jnp.dot(air_out, flux_weight, preferred_element_type=jnp.float32)
    ).astype(jnp.bfloat16)
    live_slots = (jnp.arange(slots)[None, :] < slot_counts[0][:, None]).astype(jnp.float32)
    slot_scale = (slot_area[0] * live_slots)[..., None]
    send_hot = one_hot(send_cell[0], cells)
    recv_hot = one_hot(recv_cell[0], sea_cells)
    picked = gather_rows(send_hot, flux_rows).reshape(devices, slots, sea_width)
    outgoing = (picked * slot_scale).astype(jnp.bfloat16)
    arrived = lax.all_to_all(outgoing, ("lat", "lon"), split_axis=0, concat_axis=0, tiled=True)
    coupled = scatter_rows(recv_hot, arrived.reshape(-1, sea_width))
    sea_in = ocean_state.astype(jnp.float32) + coupled
    scale_sea = lax.rsqrt(jnp.mean(sea_in * sea_in, axis=-1, keepdims=True) + 1e-06)
    sea_normed = (sea_in * scale_sea * ocean_gain).astype(jnp.bfloat16)
    sea_pre = jnp.dot(sea_normed, ocean_inner, preferred_element_type=jnp.float32)
    sea_hidden = jax.nn.silu(sea_pre).astype(jnp.bfloat16)
    sea_vdown = jnp.dot(sea_hidden.T, ocean_cot, preferred_element_type=jnp.float32)
    sea_ghid = jnp.dot(ocean_cot, ocean_outer.T, preferred_element_type=jnp.float32)
    sea_gpre = (sea_ghid * silu_slope(sea_pre)).astype(jnp.bfloat16)
    sea_vup = jnp.dot(sea_normed.T, sea_gpre, preferred_element_type=jnp.float32)
    sea_gnorm = jnp.dot(sea_gpre, ocean_inner.T, preferred_element_type=jnp.float32)
    sea_mean = jnp.mean(sea_in * ocean_gain * sea_gnorm, axis=-1, keepdims=True)
    sea_grad = (
        ocean_cot.astype(jnp.float32)
        + scale_sea * ocean_gain * sea_gnorm
        - sea_in * scale_sea**3 * sea_mean
    )
    grad_ocean = sea_grad.astype(jnp.bfloat16)
    slot_return = (
        gather_rows(recv_hot, grad_ocean).astype(jnp.bfloat16).reshape(devices, slots, sea_width)
    )
    returned = lax.all_to_all(slot_return, ("lat", "lon"), split_axis=0, concat_axis=0, tiled=True)
    addends = (returned.astype(jnp.float32) * slot_scale).reshape(-1, sea_width)
    addends_hi = addends.astype(jnp.bfloat16)
    addends_lo = (addends - addends_hi.astype(jnp.float32)).astype(jnp.bfloat16)
    flux_grad = scatter_rows(send_hot, addends_hi) + scatter_rows(send_hot, addends_lo)
    flux_masked = (sea_mask * flux_grad).astype(jnp.bfloat16)
    flux_wsum = jnp.dot(air_out.T, flux_masked, preferred_element_type=jnp.float32)
    air_grad = atmosphere_cot.reshape(cells, channels).astype(jnp.float32) + jnp.dot(
        flux_masked, flux_weight.T, preferred_element_type=jnp.float32
    )
    air_gradb = air_grad.astype(jnp.bfloat16)
    outer_sum = jnp.dot(hidden.T, air_gradb, preferred_element_type=jnp.float32)
    hid_grad = jnp.dot(air_gradb, outer_weight.T, preferred_element_type=jnp.float32)
    pre_grad = (hid_grad * silu_slope(pre)).astype(jnp.bfloat16)
    inner_sum = jnp.dot(normed.T, pre_grad, preferred_element_type=jnp.float32)
    norm_grad = jnp.dot(pre_grad, inner_weight.T, preferred_element_type=jnp.float32)
    air_mean = jnp.mean(conv_cells * atmosphere_gain * norm_grad, axis=-1, keepdims=True)
    conv_grad = (
        air_grad + scale_air * atmosphere_gain * norm_grad - conv_cells * scale_air**3 * air_mean
    ).astype(jnp.bfloat16)
    grad_extended = polar_rows(
        with_halo(conv_grad.reshape(rows, cols, channels), (("lat", 0), ("lon", 1)), DMAX), rows
    )
    grad_atmosphere = dilated(grad_extended, conv_taps, dilation, True, rows, cols).astype(
        jnp.bfloat16
    )
    summed = lax.psum(
        (
            inner_sum * air_factor,
            outer_sum * air_factor,
            flux_wsum * air_factor,
            sea_vup * sea_factor,
            sea_vdown * sea_factor,
        ),
        ("lat", "lon"),
    )
    return (grad_atmosphere, grad_ocean) + tuple(summed)


def solution(mesh):
    in_specs = (
        P("lat", "lon", None),
        P(("lat", "lon"), None),
        P(),
        P(),
        P(),
        P(),
        P(),
        P(),
        P(),
        P(),
        P(),
        P("lat", "lon"),
        P(("lat", "lon"), None, None),
        P(("lat", "lon"), None),
        P(("lat", "lon"), None, None),
        P(("lat", "lon"), None, None),
        P("lat", "lon", None),
        P(("lat", "lon"), None),
    )
    out_specs = (P("lat", "lon", None), P(("lat", "lon"), None), P(), P(), P(), P(), P())
    return jax.shard_map(local, mesh=mesh, in_specs=in_specs, out_specs=out_specs, check_vma=False)
```

```python
import jax
import jax.numpy as jnp
from jax import lax
from jax.sharding import PartitionSpec as P

DMAX = 4


def with_halo(block, sides, width):
    (lat_axis, lat_dim), (lon_axis, lon_dim) = sides
    pieces = []
    for axis, dim in sides:
        count = lax.axis_size(axis)
        forward = [(i, i + 1) for i in range(count - 1)]
        forward.append((count - 1, 0))
        backward = [(target, source) for source, target in forward]
        low = lax.ppermute(
            lax.slice_in_dim(block, block.shape[dim] - width, None, axis=dim), axis, forward
        )
        high = lax.ppermute(lax.slice_in_dim(block, 0, width, axis=dim), axis, backward)
        pieces.append((low, high))
    (south, north), (west, east) = pieces
    rows = jnp.concatenate([south, block, north], axis=lat_dim)
    pad = [(0, 0)] * block.ndim
    pad[lat_dim] = (width, width)
    west = jnp.pad(west, pad)
    east = jnp.pad(east, pad)
    return jnp.concatenate([west, rows, east], axis=lon_dim)


def one_hot(index, size):
    return (index.reshape(-1, 1) == jnp.arange(size)[None, :]).astype(jnp.bfloat16)


def gather_rows(hot, values):
    return jnp.dot(hot, values, preferred_element_type=jnp.float32)


def scatter_rows(hot, values):
    return lax.dot_general(
        hot, values, (((0,), (0,)), ((), ())), preferred_element_type=jnp.float32
    )


AXES = ("lat", "lon")
RINGS = ("x", "y", "z")


def device_of(zh, y, zl, x, core):
    return (zh * 4 + y) * 16 + zl * 8 + x * 2 + core


def all_devices():
    for zh in range(2):
        for y in range(4):
            for zl in range(2):
                for x in range(4):
                    for core in range(2):
                        yield zh, y, zl, x, core


def core_pairs():
    return [(device_of(zh, y, zl, x, c), device_of(zh, y, zl, x, 1 - c)) for zh, y, zl, x, c in all_devices()]


def ring_pairs(ring, shift):
    pairs = []
    for zh, y, zl, x, c in all_devices():
        tx, ty, tz = x, y, zh * 2 + zl
        if ring == "x":
            tx = (x + shift) % 4
        elif ring == "y":
            ty = (y + shift) % 4
        else:
            tz = (tz + shift) % 4
        pairs.append((device_of(zh, y, zl, x, c), device_of(tz // 2, ty, tz % 2, tx, c)))
    return pairs


def ring_positions():
    lat = lax.axis_index("lat")
    lon = lax.axis_index("lon")
    return {"x": (lon // 2) % 4, "y": lat % 4, "z": (lat // 4) * 2 + lon // 8}, lon % 2


def place(stack, own_at):
    gathered = jnp.zeros_like(stack)
    for s in range(stack.shape[0]):
        gathered = lax.dynamic_update_index_in_dim(gathered, stack[s], (own_at - s) % stack.shape[0], 0)
    return gathered


def tree_allreduce(parts):
    lanes = 128
    rows = [p.size // lanes for p in parts]
    data = jnp.concatenate([p.reshape(r, lanes) for p, r in zip(parts, rows)], axis=0)
    total = data.shape[0]
    unit = 2 * 64 * 8
    padded = -(-total // unit) * unit
    block = padded // (2 * 64)
    data = jnp.pad(data, ((0, padded - total), (0, 0))).reshape(2, 4, 4, 4, block, lanes)
    pos, core = ring_positions()
    mine = lax.dynamic_index_in_dim(data, core, 0, keepdims=False)
    other = lax.dynamic_index_in_dim(data, 1 - core, 0, keepdims=False)
    chunk = mine + lax.ppermute(other, AXES, core_pairs())
    for ring in RINGS:
        p = pos[ring]
        acc = lax.dynamic_index_in_dim(chunk, p, 0, keepdims=False)
        for s in range(1, 4):
            piece = lax.dynamic_index_in_dim(chunk, (p + s) % 4, 0, keepdims=False)
            acc = acc + lax.ppermute(piece.astype(jnp.bfloat16), AXES, ring_pairs(ring, s)).astype(jnp.float32)
        chunk = acc
    chunk = chunk.astype(jnp.bfloat16)
    for ring in reversed(RINGS):
        got = [chunk] + [lax.ppermute(chunk, AXES, ring_pairs(ring, s)) for s in range(1, 4)]
        chunk = place(jnp.stack(got), pos[ring])
    both = place(jnp.stack([chunk, lax.ppermute(chunk, AXES, core_pairs())]), core)
    flat = both.reshape(padded, lanes)[:total].astype(jnp.float32)
    out, at = [], 0
    for p, r in zip(parts, rows):
        out.append(flat[at : at + r].reshape(p.shape))
        at += r
    return out


def silu_slope(value):
    sig = jax.nn.sigmoid(value)
    return sig * (1.0 + value * (1.0 - sig))


def dilated(extended, conv_taps, dilation, transpose, rows, cols):
    centre = extended[DMAX : DMAX + rows, DMAX : DMAX + cols].astype(jnp.float32)
    result = conv_taps[0] * centre
    for offset in range(1, DMAX + 1):
        select = (dilation == offset).astype(jnp.float32)
        west = extended[DMAX : DMAX + rows, DMAX - offset : DMAX - offset + cols].astype(
            jnp.float32
        )
        east = extended[DMAX : DMAX + rows, DMAX + offset : DMAX + offset + cols].astype(
            jnp.float32
        )
        south = extended[DMAX - offset : DMAX - offset + rows, DMAX : DMAX + cols].astype(
            jnp.float32
        )
        north = extended[DMAX + offset : DMAX + offset + rows, DMAX : DMAX + cols].astype(
            jnp.float32
        )
        if transpose:
            west, east, south, north = (east, west, north, south)
        result = result + select * (
            conv_taps[1] * west + conv_taps[2] * east + conv_taps[3] * south + conv_taps[4] * north
        )
    return result


def dilated_once(extended, conv_taps, dilation, rows, cols):
    centre = extended[DMAX : DMAX + rows, DMAX : DMAX + cols].astype(jnp.float32)
    sides = []
    for row_at, col_at in ((0, -1), (0, 1), (-1, 0), (1, 0)):
        picked = None
        for offset in range(DMAX, 0, -1):
            r0 = DMAX + row_at * offset
            c0 = DMAX + col_at * offset
            window = extended[r0 : r0 + rows, c0 : c0 + cols].astype(jnp.float32)
            picked = window if picked is None else jnp.where(dilation == offset, window, picked)
        sides.append(picked)
    west, east, south, north = sides
    return conv_taps[0] * centre + (
        conv_taps[1] * west + conv_taps[2] * east + conv_taps[3] * south + conv_taps[4] * north
    )


def polar_rows(extended, rows):
    band_rows = lax.axis_index("lat") * rows + jnp.arange(-DMAX, rows + DMAX)
    inside = (band_rows >= 0) & (band_rows < lax.axis_size("lat") * rows)
    return extended * inside[:, None, None].astype(extended.dtype)


def local(
    atmosphere,
    ocean_state,
    dilation,
    conv_taps,
    atmosphere_gain,
    ocean_gain,
    inner_weight,
    outer_weight,
    flux_weight,
    ocean_inner,
    ocean_outer,
    land_sea,
    send_cell,
    slot_counts,
    slot_area,
    recv_cell,
    atmosphere_cot,
    ocean_cot,
):
    rows, cols, channels = atmosphere.shape
    cells = rows * cols
    lat_count = lax.axis_size("lat")
    lon_count = lax.axis_size("lon")
    devices = lat_count * lon_count
    slots = send_cell.shape[2]
    sea_width = flux_weight.shape[1]
    sea_cells = ocean_state.shape[0]
    air_factor = float(cells * devices) ** (-0.5)
    sea_factor = float(sea_cells * devices) ** (-0.5)
    extended = polar_rows(with_halo(atmosphere, (("lat", 0), ("lon", 1)), DMAX), rows)
    conv_cells = lax.optimization_barrier(
        dilated_once(extended, conv_taps, dilation, rows, cols).reshape(cells, channels)
    )
    scale_air = lax.rsqrt(jnp.mean(conv_cells * conv_cells, axis=-1, keepdims=True) + 1e-06)
    normed = (conv_cells * scale_air * atmosphere_gain).astype(jnp.bfloat16)
    pre = jnp.dot(normed, inner_weight, preferred_element_type=jnp.float32)
    hidden = jax.nn.silu(pre).astype(jnp.bfloat16)
    air_out = (
        conv_cells + jnp.dot(hidden, outer_weight, preferred_element_type=jnp.float32)
    ).astype(jnp.bfloat16)
    sea_mask = land_sea.reshape(cells, 1).astype(jnp.float32)
    flux_rows = (
        sea_mask * jnp.dot(air_out, flux_weight, preferred_element_type=jnp.float32)
    ).astype(jnp.bfloat16)
    live_slots = (jnp.arange(slots)[None, :] < slot_counts[0][:, None]).astype(jnp.float32)
    slot_scale = (slot_area[0] * live_slots)[..., None]
    send_hot = one_hot(send_cell[0], cells)
    recv_hot = one_hot(recv_cell[0], sea_cells)
    picked = gather_rows(send_hot, flux_rows).reshape(devices, slots, sea_width)
    outgoing = (picked * slot_scale).astype(jnp.bfloat16)
    arrived = lax.all_to_all(outgoing, ("lat", "lon"), split_axis=0, concat_axis=0, tiled=True)
    coupled = scatter_rows(recv_hot, arrived.reshape(-1, sea_width))
    sea_in = ocean_state.astype(jnp.float32) + coupled
    scale_sea = lax.rsqrt(jnp.mean(sea_in * sea_in, axis=-1, keepdims=True) + 1e-06)
    sea_normed = (sea_in * scale_sea * ocean_gain).astype(jnp.bfloat16)
    sea_pre = jnp.dot(sea_normed, ocean_inner, preferred_element_type=jnp.float32)
    sea_hidden = jax.nn.silu(sea_pre).astype(jnp.bfloat16)
    sea_vdown = jnp.dot(sea_hidden.T, ocean_cot, preferred_element_type=jnp.float32)
    sea_ghid = jnp.dot(ocean_cot, ocean_outer.T, preferred_element_type=jnp.float32)
    sea_gpre = (sea_ghid * silu_slope(sea_pre)).astype(jnp.bfloat16)
    sea_vup = jnp.dot(sea_normed.T, sea_gpre, preferred_element_type=jnp.float32)
    sea_gnorm = jnp.dot(sea_gpre, ocean_inner.T, preferred_element_type=jnp.float32)
    sea_mean = jnp.mean(sea_in * ocean_gain * sea_gnorm, axis=-1, keepdims=True)
    sea_grad = (
        ocean_cot.astype(jnp.float32)
        + scale_sea * ocean_gain * sea_gnorm
        - sea_in * scale_sea**3 * sea_mean
    )
    grad_ocean = sea_grad.astype(jnp.bfloat16)
    slot_return = (
        gather_rows(recv_hot, grad_ocean).astype(jnp.bfloat16).reshape(devices, slots, sea_width)
    )
    returned = lax.all_to_all(slot_return, ("lat", "lon"), split_axis=0, concat_axis=0, tiled=True)
    addends = (returned.astype(jnp.float32) * slot_scale).reshape(-1, sea_width)
    addends_hi = addends.astype(jnp.bfloat16)
    addends_lo = (addends - addends_hi.astype(jnp.float32)).astype(jnp.bfloat16)
    flux_grad = scatter_rows(send_hot, addends_hi) + scatter_rows(send_hot, addends_lo)
    flux_masked = (sea_mask * flux_grad).astype(jnp.bfloat16)
    flux_wsum = jnp.dot(air_out.T, flux_masked, preferred_element_type=jnp.float32)
    air_grad = atmosphere_cot.reshape(cells, channels).astype(jnp.float32) + jnp.dot(
        flux_masked, flux_weight.T, preferred_element_type=jnp.float32
    )
    air_gradb = air_grad.astype(jnp.bfloat16)
    outer_sum = jnp.dot(hidden.T, air_gradb, preferred_element_type=jnp.float32)
    hid_grad = jnp.dot(air_gradb, outer_weight.T, preferred_element_type=jnp.float32)
    pre_grad = (hid_grad * silu_slope(pre)).astype(jnp.bfloat16)
    inner_sum = jnp.dot(normed.T, pre_grad, preferred_element_type=jnp.float32)
    norm_grad = jnp.dot(pre_grad, inner_weight.T, preferred_element_type=jnp.float32)
    air_mean = jnp.mean(conv_cells * atmosphere_gain * norm_grad, axis=-1, keepdims=True)
    conv_grad = (
        air_grad + scale_air * atmosphere_gain * norm_grad - conv_cells * scale_air**3 * air_mean
    ).astype(jnp.bfloat16)
    grad_extended = polar_rows(
        with_halo(conv_grad.reshape(rows, cols, channels), (("lat", 0), ("lon", 1)), DMAX), rows
    )
    grad_atmosphere = dilated(grad_extended, conv_taps, dilation, True, rows, cols).astype(
        jnp.bfloat16
    )
    summed = tree_allreduce(
        (
            inner_sum * air_factor,
            outer_sum * air_factor,
            flux_wsum * air_factor,
            sea_vup * sea_factor,
            sea_vdown * sea_factor,
        )
    )
    return (grad_atmosphere, grad_ocean) + tuple(summed)


def solution(mesh):
    in_specs = (
        P("lat", "lon", None),
        P(("lat", "lon"), None),
        P(),
        P(),
        P(),
        P(),
        P(),
        P(),
        P(),
        P(),
        P(),
        P("lat", "lon"),
        P(("lat", "lon"), None, None),
        P(("lat", "lon"), None),
        P(("lat", "lon"), None, None),
        P(("lat", "lon"), None, None),
        P("lat", "lon", None),
        P(("lat", "lon"), None),
    )
    out_specs = (P("lat", "lon", None), P(("lat", "lon"), None), P(), P(), P(), P(), P())
    return jax.shard_map(local, mesh=mesh, in_specs=in_specs, out_specs=out_specs, check_vma=False)
```

```python
import jax
import jax.numpy as jnp
from jax import lax
from jax.sharding import PartitionSpec as P

DMAX = 4


def with_halo(block, sides, width):
    (lat_axis, lat_dim), (lon_axis, lon_dim) = sides
    pieces = []
    for axis, dim in sides:
        count = lax.axis_size(axis)
        forward = [(i, i + 1) for i in range(count - 1)]
        forward.append((count - 1, 0))
        backward = [(target, source) for source, target in forward]
        low = lax.ppermute(
            lax.slice_in_dim(block, block.shape[dim] - width, None, axis=dim), axis, forward
        )
        high = lax.ppermute(lax.slice_in_dim(block, 0, width, axis=dim), axis, backward)
        pieces.append((low, high))
    (south, north), (west, east) = pieces
    rows = jnp.concatenate([south, block, north], axis=lat_dim)
    pad = [(0, 0)] * block.ndim
    pad[lat_dim] = (width, width)
    west = jnp.pad(west, pad)
    east = jnp.pad(east, pad)
    return jnp.concatenate([west, rows, east], axis=lon_dim)


def one_hot(index, size):
    return (index.reshape(-1, 1) == jnp.arange(size)[None, :]).astype(jnp.bfloat16)


def gather_rows(hot, values):
    return jnp.dot(hot, values, preferred_element_type=jnp.float32)


def scatter_rows(hot, values):
    return lax.dot_general(
        hot, values, (((0,), (0,)), ((), ())), preferred_element_type=jnp.float32
    )


AXES = ("lat", "lon")
RINGS = ("x", "y", "z")


def device_of(zh, y, zl, x, core):
    return (zh * 4 + y) * 16 + zl * 8 + x * 2 + core


def all_devices():
    for zh in range(2):
        for y in range(4):
            for zl in range(2):
                for x in range(4):
                    for core in range(2):
                        yield zh, y, zl, x, core


def core_pairs():
    return [(device_of(zh, y, zl, x, c), device_of(zh, y, zl, x, 1 - c)) for zh, y, zl, x, c in all_devices()]


def ring_pairs(ring, shift):
    pairs = []
    for zh, y, zl, x, c in all_devices():
        tx, ty, tz = x, y, zh * 2 + zl
        if ring == "x":
            tx = (x + shift) % 4
        elif ring == "y":
            ty = (y + shift) % 4
        else:
            tz = (tz + shift) % 4
        pairs.append((device_of(zh, y, zl, x, c), device_of(tz // 2, ty, tz % 2, tx, c)))
    return pairs


def ring_positions():
    lat = lax.axis_index("lat")
    lon = lax.axis_index("lon")
    return {"x": (lon // 2) % 4, "y": lat % 4, "z": (lat // 4) * 2 + lon // 8}, lon % 2


def place(stack, own_at):
    gathered = jnp.zeros_like(stack)
    for s in range(stack.shape[0]):
        gathered = lax.dynamic_update_index_in_dim(gathered, stack[s], (own_at - s) % stack.shape[0], 0)
    return gathered


def tiles_of(matrix):
    rows, cols = matrix.shape
    return matrix.reshape(rows // 8, 8, cols // 128, 128).transpose(0, 2, 1, 3).reshape(-1, 128)


def from_tiles(packed, shape):
    rows, cols = shape
    return packed.reshape(rows // 8, cols // 128, 8, 128).transpose(0, 2, 1, 3).reshape(rows, cols)


def tree_allreduce(parts):
    lanes = 128
    rows = [p.size // lanes for p in parts]
    data = jnp.concatenate([tiles_of(p) for p in parts], axis=0)
    total = data.shape[0]
    unit = 2 * 64 * 8
    padded = -(-total // unit) * unit
    block = padded // (2 * 64)
    data = jnp.pad(data, ((0, padded - total), (0, 0))).reshape(2, 4, 4, 4, block, lanes)
    pos, core = ring_positions()
    mine = lax.dynamic_index_in_dim(data, core, 0, keepdims=False)
    other = lax.dynamic_index_in_dim(data, 1 - core, 0, keepdims=False)
    chunk = mine + lax.ppermute(other, AXES, core_pairs())
    for ring in RINGS:
        p = pos[ring]
        acc = lax.dynamic_index_in_dim(chunk, p, 0, keepdims=False)
        for s in range(1, 4):
            piece = lax.dynamic_index_in_dim(chunk, (p + s) % 4, 0, keepdims=False)
            acc = acc + lax.ppermute(piece.astype(jnp.bfloat16), AXES, ring_pairs(ring, s)).astype(jnp.float32)
        chunk = acc
    chunk = chunk.astype(jnp.bfloat16)
    for ring in reversed(RINGS):
        got = [chunk] + [lax.ppermute(chunk, AXES, ring_pairs(ring, s)) for s in range(1, 4)]
        chunk = place(jnp.stack(got), pos[ring])
    both = place(jnp.stack([chunk, lax.ppermute(chunk, AXES, core_pairs())]), core)
    flat = both.reshape(padded, lanes)[:total].astype(jnp.float32)
    out, at = [], 0
    for p, r in zip(parts, rows):
        out.append(from_tiles(flat[at : at + r], p.shape))
        at += r
    return out


def silu_slope(value):
    sig = jax.nn.sigmoid(value)
    return sig * (1.0 + value * (1.0 - sig))


def dilated(extended, conv_taps, dilation, transpose, rows, cols):
    centre = extended[DMAX : DMAX + rows, DMAX : DMAX + cols].astype(jnp.float32)
    result = conv_taps[0] * centre
    for offset in range(1, DMAX + 1):
        select = (dilation == offset).astype(jnp.float32)
        west = extended[DMAX : DMAX + rows, DMAX - offset : DMAX - offset + cols].astype(
            jnp.float32
        )
        east = extended[DMAX : DMAX + rows, DMAX + offset : DMAX + offset + cols].astype(
            jnp.float32
        )
        south = extended[DMAX - offset : DMAX - offset + rows, DMAX : DMAX + cols].astype(
            jnp.float32
        )
        north = extended[DMAX + offset : DMAX + offset + rows, DMAX : DMAX + cols].astype(
            jnp.float32
        )
        if transpose:
            west, east, south, north = (east, west, north, south)
        result = result + select * (
            conv_taps[1] * west + conv_taps[2] * east + conv_taps[3] * south + conv_taps[4] * north
        )
    return result


def dilated_once(extended, conv_taps, dilation, rows, cols):
    centre = extended[DMAX : DMAX + rows, DMAX : DMAX + cols].astype(jnp.float32)
    sides = []
    for row_at, col_at in ((0, -1), (0, 1), (-1, 0), (1, 0)):
        picked = None
        for offset in range(DMAX, 0, -1):
            r0 = DMAX + row_at * offset
            c0 = DMAX + col_at * offset
            window = extended[r0 : r0 + rows, c0 : c0 + cols].astype(jnp.float32)
            picked = window if picked is None else jnp.where(dilation == offset, window, picked)
        sides.append(picked)
    west, east, south, north = sides
    return conv_taps[0] * centre + (
        conv_taps[1] * west + conv_taps[2] * east + conv_taps[3] * south + conv_taps[4] * north
    )


def polar_rows(extended, rows):
    band_rows = lax.axis_index("lat") * rows + jnp.arange(-DMAX, rows + DMAX)
    inside = (band_rows >= 0) & (band_rows < lax.axis_size("lat") * rows)
    return extended * inside[:, None, None].astype(extended.dtype)


def local(
    atmosphere,
    ocean_state,
    dilation,
    conv_taps,
    atmosphere_gain,
    ocean_gain,
    inner_weight,
    outer_weight,
    flux_weight,
    ocean_inner,
    ocean_outer,
    land_sea,
    send_cell,
    slot_counts,
    slot_area,
    recv_cell,
    atmosphere_cot,
    ocean_cot,
):
    rows, cols, channels = atmosphere.shape
    cells = rows * cols
    lat_count = lax.axis_size("lat")
    lon_count = lax.axis_size("lon")
    devices = lat_count * lon_count
    slots = send_cell.shape[2]
    sea_width = flux_weight.shape[1]
    sea_cells = ocean_state.shape[0]
    air_factor = float(cells * devices) ** (-0.5)
    sea_factor = float(sea_cells * devices) ** (-0.5)
    extended = polar_rows(with_halo(atmosphere, (("lat", 0), ("lon", 1)), DMAX), rows)
    conv_cells = lax.optimization_barrier(
        dilated_once(extended, conv_taps, dilation, rows, cols).reshape(cells, channels)
    )
    scale_air = lax.rsqrt(jnp.mean(conv_cells * conv_cells, axis=-1, keepdims=True) + 1e-06)
    normed = (conv_cells * scale_air * atmosphere_gain).astype(jnp.bfloat16)
    pre = jnp.dot(normed, inner_weight, preferred_element_type=jnp.float32)
    hidden = jax.nn.silu(pre).astype(jnp.bfloat16)
    air_out = (
        conv_cells + jnp.dot(hidden, outer_weight, preferred_element_type=jnp.float32)
    ).astype(jnp.bfloat16)
    sea_mask = land_sea.reshape(cells, 1).astype(jnp.float32)
    flux_rows = (
        sea_mask * jnp.dot(air_out, flux_weight, preferred_element_type=jnp.float32)
    ).astype(jnp.bfloat16)
    live_slots = (jnp.arange(slots)[None, :] < slot_counts[0][:, None]).astype(jnp.float32)
    slot_scale = (slot_area[0] * live_slots)[..., None]
    send_hot = one_hot(send_cell[0], cells)
    recv_hot = one_hot(recv_cell[0], sea_cells)
    picked = gather_rows(send_hot, flux_rows).reshape(devices, slots, sea_width)
    outgoing = (picked * slot_scale).astype(jnp.bfloat16)
    arrived = lax.all_to_all(outgoing, ("lat", "lon"), split_axis=0, concat_axis=0, tiled=True)
    coupled = scatter_rows(recv_hot, arrived.reshape(-1, sea_width))
    sea_in = ocean_state.astype(jnp.float32) + coupled
    scale_sea = lax.rsqrt(jnp.mean(sea_in * sea_in, axis=-1, keepdims=True) + 1e-06)
    sea_normed = (sea_in * scale_sea * ocean_gain).astype(jnp.bfloat16)
    sea_pre = jnp.dot(sea_normed, ocean_inner, preferred_element_type=jnp.float32)
    sea_hidden = jax.nn.silu(sea_pre).astype(jnp.bfloat16)
    sea_vdown = jnp.dot(sea_hidden.T, ocean_cot, preferred_element_type=jnp.float32)
    sea_ghid = jnp.dot(ocean_cot, ocean_outer.T, preferred_element_type=jnp.float32)
    sea_gpre = (sea_ghid * silu_slope(sea_pre)).astype(jnp.bfloat16)
    sea_vup = jnp.dot(sea_normed.T, sea_gpre, preferred_element_type=jnp.float32)
    sea_gnorm = jnp.dot(sea_gpre, ocean_inner.T, preferred_element_type=jnp.float32)
    sea_mean = jnp.mean(sea_in * ocean_gain * sea_gnorm, axis=-1, keepdims=True)
    sea_grad = (
        ocean_cot.astype(jnp.float32)
        + scale_sea * ocean_gain * sea_gnorm
        - sea_in * scale_sea**3 * sea_mean
    )
    grad_ocean = sea_grad.astype(jnp.bfloat16)
    slot_return = (
        gather_rows(recv_hot, grad_ocean).astype(jnp.bfloat16).reshape(devices, slots, sea_width)
    )
    returned = lax.all_to_all(slot_return, ("lat", "lon"), split_axis=0, concat_axis=0, tiled=True)
    addends = (returned.astype(jnp.float32) * slot_scale).reshape(-1, sea_width)
    addends_hi = addends.astype(jnp.bfloat16)
    addends_lo = (addends - addends_hi.astype(jnp.float32)).astype(jnp.bfloat16)
    flux_grad = scatter_rows(send_hot, addends_hi) + scatter_rows(send_hot, addends_lo)
    flux_masked = (sea_mask * flux_grad).astype(jnp.bfloat16)
    flux_wsum = jnp.dot(air_out.T, flux_masked, preferred_element_type=jnp.float32)
    air_grad = atmosphere_cot.reshape(cells, channels).astype(jnp.float32) + jnp.dot(
        flux_masked, flux_weight.T, preferred_element_type=jnp.float32
    )
    air_gradb = air_grad.astype(jnp.bfloat16)
    outer_sum = jnp.dot(hidden.T, air_gradb, preferred_element_type=jnp.float32)
    hid_grad = jnp.dot(air_gradb, outer_weight.T, preferred_element_type=jnp.float32)
    pre_grad = (hid_grad * silu_slope(pre)).astype(jnp.bfloat16)
    inner_sum = jnp.dot(normed.T, pre_grad, preferred_element_type=jnp.float32)
    norm_grad = jnp.dot(pre_grad, inner_weight.T, preferred_element_type=jnp.float32)
    air_mean = jnp.mean(conv_cells * atmosphere_gain * norm_grad, axis=-1, keepdims=True)
    conv_grad = (
        air_grad + scale_air * atmosphere_gain * norm_grad - conv_cells * scale_air**3 * air_mean
    ).astype(jnp.bfloat16)
    grad_extended = polar_rows(
        with_halo(conv_grad.reshape(rows, cols, channels), (("lat", 0), ("lon", 1)), DMAX), rows
    )
    grad_atmosphere = dilated(grad_extended, conv_taps, dilation, True, rows, cols).astype(
        jnp.bfloat16
    )
    summed = tree_allreduce(
        (
            inner_sum * air_factor,
            outer_sum * air_factor,
            flux_wsum * air_factor,
            sea_vup * sea_factor,
            sea_vdown * sea_factor,
        )
    )
    return (grad_atmosphere, grad_ocean) + tuple(summed)


def solution(mesh):
    in_specs = (
        P("lat", "lon", None),
        P(("lat", "lon"), None),
        P(),
        P(),
        P(),
        P(),
        P(),
        P(),
        P(),
        P(),
        P(),
        P("lat", "lon"),
        P(("lat", "lon"), None, None),
        P(("lat", "lon"), None),
        P(("lat", "lon"), None, None),
        P(("lat", "lon"), None, None),
        P("lat", "lon", None),
        P(("lat", "lon"), None),
    )
    out_specs = (P("lat", "lon", None), P(("lat", "lon"), None), P(), P(), P(), P(), P())
    return jax.shard_map(local, mesh=mesh, in_specs=in_specs, out_specs=out_specs, check_vma=False)
```

```python
import jax
import jax.numpy as jnp
from jax import lax
from jax.sharding import PartitionSpec as P

DMAX = 4


def with_halo(block, sides, width):
    (lat_axis, lat_dim), (lon_axis, lon_dim) = sides
    pieces = []
    for axis, dim in sides:
        count = lax.axis_size(axis)
        forward = [(i, i + 1) for i in range(count - 1)]
        forward.append((count - 1, 0))
        backward = [(target, source) for source, target in forward]
        low = lax.ppermute(
            lax.slice_in_dim(block, block.shape[dim] - width, None, axis=dim), axis, forward
        )
        high = lax.ppermute(lax.slice_in_dim(block, 0, width, axis=dim), axis, backward)
        pieces.append((low, high))
    (south, north), (west, east) = pieces
    rows = jnp.concatenate([south, block, north], axis=lat_dim)
    pad = [(0, 0)] * block.ndim
    pad[lat_dim] = (width, width)
    west = jnp.pad(west, pad)
    east = jnp.pad(east, pad)
    return jnp.concatenate([west, rows, east], axis=lon_dim)


def one_hot(index, size):
    return (index.reshape(-1, 1) == jnp.arange(size)[None, :]).astype(jnp.bfloat16)


def gather_rows(hot, values):
    return jnp.dot(hot, values, preferred_element_type=jnp.float32)


def scatter_rows(hot, values):
    return lax.dot_general(
        hot, values, (((0,), (0,)), ((), ())), preferred_element_type=jnp.float32
    )


AXES = ("lat", "lon")
RINGS = ("x", "y", "z")


def device_of(zh, y, zl, x, core):
    return (zh * 4 + y) * 16 + zl * 8 + x * 2 + core


def all_devices():
    for zh in range(2):
        for y in range(4):
            for zl in range(2):
                for x in range(4):
                    for core in range(2):
                        yield zh, y, zl, x, core


def core_pairs():
    return [(device_of(zh, y, zl, x, c), device_of(zh, y, zl, x, 1 - c)) for zh, y, zl, x, c in all_devices()]


def ring_pairs(ring, shift):
    pairs = []
    for zh, y, zl, x, c in all_devices():
        tx, ty, tz = x, y, zh * 2 + zl
        if ring == "x":
            tx = (x + shift) % 4
        elif ring == "y":
            ty = (y + shift) % 4
        else:
            tz = (tz + shift) % 4
        pairs.append((device_of(zh, y, zl, x, c), device_of(tz // 2, ty, tz % 2, tx, c)))
    return pairs


def ring_positions():
    lat = lax.axis_index("lat")
    lon = lax.axis_index("lon")
    return {"x": (lon // 2) % 4, "y": lat % 4, "z": (lat // 4) * 2 + lon // 8}, lon % 2


def place(stack, own_at):
    gathered = jnp.zeros_like(stack)
    for s in range(stack.shape[0]):
        gathered = lax.dynamic_update_index_in_dim(gathered, stack[s], (own_at - s) % stack.shape[0], 0)
    return gathered


def tiles_of(matrix):
    rows, cols = matrix.shape
    return matrix.reshape(rows // 8, 8, cols // 128, 128).transpose(0, 2, 1, 3).reshape(-1, 128)


def from_tiles(packed, shape):
    rows, cols = shape
    return packed.reshape(rows // 8, cols // 128, 8, 128).transpose(0, 2, 1, 3).reshape(rows, cols)


def tree_allreduce(parts, after):
    lanes = 128
    rows = [p.size // lanes for p in parts]
    data = jnp.concatenate([tiles_of(p) for p in parts], axis=0)
    total = data.shape[0]
    unit = 2 * 64 * 8
    padded = -(-total // unit) * unit
    block = padded // (2 * 64)
    data = jnp.pad(data, ((0, padded - total), (0, 0))).reshape(2, 4, 4, 4, block, lanes)
    pos, core = ring_positions()
    mine = lax.dynamic_index_in_dim(data, core, 0, keepdims=False)
    other = lax.dynamic_index_in_dim(data, 1 - core, 0, keepdims=False)
    chunk = mine + lax.ppermute(other, AXES, core_pairs())
    for ring in RINGS:
        if ring == "y":
            chunk = chunk + after
        p = pos[ring]
        acc = lax.dynamic_index_in_dim(chunk, p, 0, keepdims=False)
        for s in range(1, 4):
            piece = lax.dynamic_index_in_dim(chunk, (p + s) % 4, 0, keepdims=False)
            acc = acc + lax.ppermute(piece.astype(jnp.bfloat16), AXES, ring_pairs(ring, s)).astype(jnp.float32)
        chunk = acc
    chunk = chunk.astype(jnp.bfloat16)
    for ring in reversed(RINGS):
        got = [chunk] + [lax.ppermute(chunk, AXES, ring_pairs(ring, s)) for s in range(1, 4)]
        chunk = place(jnp.stack(got), pos[ring])
    both = place(jnp.stack([chunk, lax.ppermute(chunk, AXES, core_pairs())]), core)
    flat = both.reshape(padded, lanes)[:total].astype(jnp.float32)
    out, at = [], 0
    for p, r in zip(parts, rows):
        out.append(from_tiles(flat[at : at + r], p.shape))
        at += r
    return out


def silu_slope(value):
    sig = jax.nn.sigmoid(value)
    return sig * (1.0 + value * (1.0 - sig))


def dilated(extended, conv_taps, dilation, transpose, rows, cols):
    centre = extended[DMAX : DMAX + rows, DMAX : DMAX + cols].astype(jnp.float32)
    result = conv_taps[0] * centre
    for offset in range(1, DMAX + 1):
        select = (dilation == offset).astype(jnp.float32)
        west = extended[DMAX : DMAX + rows, DMAX - offset : DMAX - offset + cols].astype(
            jnp.float32
        )
        east = extended[DMAX : DMAX + rows, DMAX + offset : DMAX + offset + cols].astype(
            jnp.float32
        )
        south = extended[DMAX - offset : DMAX - offset + rows, DMAX : DMAX + cols].astype(
            jnp.float32
        )
        north = extended[DMAX + offset : DMAX + offset + rows, DMAX : DMAX + cols].astype(
            jnp.float32
        )
        if transpose:
            west, east, south, north = (east, west, north, south)
        result = result + select * (
            conv_taps[1] * west + conv_taps[2] * east + conv_taps[3] * south + conv_taps[4] * north
        )
    return result


def dilated_once(extended, conv_taps, dilation, rows, cols):
    centre = extended[DMAX : DMAX + rows, DMAX : DMAX + cols].astype(jnp.float32)
    sides = []
    for row_at, col_at in ((0, -1), (0, 1), (-1, 0), (1, 0)):
        picked = None
        for offset in range(DMAX, 0, -1):
            r0 = DMAX + row_at * offset
            c0 = DMAX + col_at * offset
            window = extended[r0 : r0 + rows, c0 : c0 + cols].astype(jnp.float32)
            picked = window if picked is None else jnp.where(dilation == offset, window, picked)
        sides.append(picked)
    west, east, south, north = sides
    return conv_taps[0] * centre + (
        conv_taps[1] * west + conv_taps[2] * east + conv_taps[3] * south + conv_taps[4] * north
    )


def polar_rows(extended, rows):
    band_rows = lax.axis_index("lat") * rows + jnp.arange(-DMAX, rows + DMAX)
    inside = (band_rows >= 0) & (band_rows < lax.axis_size("lat") * rows)
    return extended * inside[:, None, None].astype(extended.dtype)


def local(
    atmosphere,
    ocean_state,
    dilation,
    conv_taps,
    atmosphere_gain,
    ocean_gain,
    inner_weight,
    outer_weight,
    flux_weight,
    ocean_inner,
    ocean_outer,
    land_sea,
    send_cell,
    slot_counts,
    slot_area,
    recv_cell,
    atmosphere_cot,
    ocean_cot,
):
    rows, cols, channels = atmosphere.shape
    cells = rows * cols
    lat_count = lax.axis_size("lat")
    lon_count = lax.axis_size("lon")
    devices = lat_count * lon_count
    slots = send_cell.shape[2]
    sea_width = flux_weight.shape[1]
    sea_cells = ocean_state.shape[0]
    air_factor = float(cells * devices) ** (-0.5)
    sea_factor = float(sea_cells * devices) ** (-0.5)
    extended = polar_rows(with_halo(atmosphere, (("lat", 0), ("lon", 1)), DMAX), rows)
    conv_cells = lax.optimization_barrier(
        dilated_once(extended, conv_taps, dilation, rows, cols).reshape(cells, channels)
    )
    scale_air = lax.rsqrt(jnp.mean(conv_cells * conv_cells, axis=-1, keepdims=True) + 1e-06)
    normed = (conv_cells * scale_air * atmosphere_gain).astype(jnp.bfloat16)
    pre = jnp.dot(normed, inner_weight, preferred_element_type=jnp.float32)
    hidden = jax.nn.silu(pre).astype(jnp.bfloat16)
    air_out = (
        conv_cells + jnp.dot(hidden, outer_weight, preferred_element_type=jnp.float32)
    ).astype(jnp.bfloat16)
    sea_mask = land_sea.reshape(cells, 1).astype(jnp.float32)
    flux_rows = (
        sea_mask * jnp.dot(air_out, flux_weight, preferred_element_type=jnp.float32)
    ).astype(jnp.bfloat16)
    live_slots = (jnp.arange(slots)[None, :] < slot_counts[0][:, None]).astype(jnp.float32)
    slot_scale = (slot_area[0] * live_slots)[..., None]
    send_hot = one_hot(send_cell[0], cells)
    recv_hot = one_hot(recv_cell[0], sea_cells)
    picked = gather_rows(send_hot, flux_rows).reshape(devices, slots, sea_width)
    outgoing = (picked * slot_scale).astype(jnp.bfloat16)
    arrived = lax.all_to_all(outgoing, ("lat", "lon"), split_axis=0, concat_axis=0, tiled=True)
    coupled = scatter_rows(recv_hot, arrived.reshape(-1, sea_width))
    sea_in = ocean_state.astype(jnp.float32) + coupled
    scale_sea = lax.rsqrt(jnp.mean(sea_in * sea_in, axis=-1, keepdims=True) + 1e-06)
    sea_normed = (sea_in * scale_sea * ocean_gain).astype(jnp.bfloat16)
    sea_pre = jnp.dot(sea_normed, ocean_inner, preferred_element_type=jnp.float32)
    sea_hidden = jax.nn.silu(sea_pre).astype(jnp.bfloat16)
    sea_vdown = jnp.dot(sea_hidden.T, ocean_cot, preferred_element_type=jnp.float32)
    sea_ghid = jnp.dot(ocean_cot, ocean_outer.T, preferred_element_type=jnp.float32)
    sea_gpre = (sea_ghid * silu_slope(sea_pre)).astype(jnp.bfloat16)
    sea_vup = jnp.dot(sea_normed.T, sea_gpre, preferred_element_type=jnp.float32)
    sea_gnorm = jnp.dot(sea_gpre, ocean_inner.T, preferred_element_type=jnp.float32)
    sea_mean = jnp.mean(sea_in * ocean_gain * sea_gnorm, axis=-1, keepdims=True)
    sea_grad = (
        ocean_cot.astype(jnp.float32)
        + scale_sea * ocean_gain * sea_gnorm
        - sea_in * scale_sea**3 * sea_mean
    )
    grad_ocean = sea_grad.astype(jnp.bfloat16)
    slot_return = (
        gather_rows(recv_hot, grad_ocean).astype(jnp.bfloat16).reshape(devices, slots, sea_width)
    )
    returned = lax.all_to_all(slot_return, ("lat", "lon"), split_axis=0, concat_axis=0, tiled=True)
    addends = (returned.astype(jnp.float32) * slot_scale).reshape(-1, sea_width)
    addends_hi = addends.astype(jnp.bfloat16)
    addends_lo = (addends - addends_hi.astype(jnp.float32)).astype(jnp.bfloat16)
    flux_grad = scatter_rows(send_hot, addends_hi) + scatter_rows(send_hot, addends_lo)
    flux_masked = (sea_mask * flux_grad).astype(jnp.bfloat16)
    flux_wsum = jnp.dot(air_out.T, flux_masked, preferred_element_type=jnp.float32)
    air_grad = atmosphere_cot.reshape(cells, channels).astype(jnp.float32) + jnp.dot(
        flux_masked, flux_weight.T, preferred_element_type=jnp.float32
    )
    air_gradb = air_grad.astype(jnp.bfloat16)
    outer_sum = jnp.dot(hidden.T, air_gradb, preferred_element_type=jnp.float32)
    hid_grad = jnp.dot(air_gradb, outer_weight.T, preferred_element_type=jnp.float32)
    pre_grad = (hid_grad * silu_slope(pre)).astype(jnp.bfloat16)
    inner_sum = jnp.dot(normed.T, pre_grad, preferred_element_type=jnp.float32)
    norm_grad = jnp.dot(pre_grad, inner_weight.T, preferred_element_type=jnp.float32)
    air_mean = jnp.mean(conv_cells * atmosphere_gain * norm_grad, axis=-1, keepdims=True)
    conv_grad = (
        air_grad + scale_air * atmosphere_gain * norm_grad - conv_cells * scale_air**3 * air_mean
    ).astype(jnp.bfloat16)
    grad_extended = polar_rows(
        with_halo(conv_grad.reshape(rows, cols, channels), (("lat", 0), ("lon", 1)), DMAX), rows
    )
    grad_stencil = dilated(grad_extended, conv_taps, dilation, True, rows, cols)
    grad_atmosphere = grad_stencil.astype(jnp.bfloat16)
    summed = tree_allreduce(
        (
            inner_sum * air_factor,
            outer_sum * air_factor,
            flux_wsum * air_factor,
            sea_vup * sea_factor,
            sea_vdown * sea_factor,
        ),
        grad_stencil[0, 0, 0] * 0.0,
    )
    return (grad_atmosphere, grad_ocean) + tuple(summed)


def solution(mesh):
    in_specs = (
        P("lat", "lon", None),
        P(("lat", "lon"), None),
        P(),
        P(),
        P(),
        P(),
        P(),
        P(),
        P(),
        P(),
        P(),
        P("lat", "lon"),
        P(("lat", "lon"), None, None),
        P(("lat", "lon"), None),
        P(("lat", "lon"), None, None),
        P(("lat", "lon"), None, None),
        P("lat", "lon", None),
        P(("lat", "lon"), None),
    )
    out_specs = (P("lat", "lon", None), P(("lat", "lon"), None), P(), P(), P(), P(), P())
    return jax.shard_map(local, mesh=mesh, in_specs=in_specs, out_specs=out_specs, check_vma=False)
```

```python
import jax
import jax.numpy as jnp
from jax import lax
from jax.sharding import PartitionSpec as P

DMAX = 4


def with_halo(block, sides, width):
    (lat_axis, lat_dim), (lon_axis, lon_dim) = sides
    pieces = []
    for axis, dim in sides:
        count = lax.axis_size(axis)
        forward = [(i, i + 1) for i in range(count - 1)]
        forward.append((count - 1, 0))
        backward = [(target, source) for source, target in forward]
        low = lax.ppermute(
            lax.slice_in_dim(block, block.shape[dim] - width, None, axis=dim), axis, forward
        )
        high = lax.ppermute(lax.slice_in_dim(block, 0, width, axis=dim), axis, backward)
        pieces.append((low, high))
    (south, north), (west, east) = pieces
    rows = jnp.concatenate([south, block, north], axis=lat_dim)
    pad = [(0, 0)] * block.ndim
    pad[lat_dim] = (width, width)
    west = jnp.pad(west, pad)
    east = jnp.pad(east, pad)
    return jnp.concatenate([west, rows, east], axis=lon_dim)


def one_hot(index, size):
    return (index.reshape(-1, 1) == jnp.arange(size)[None, :]).astype(jnp.bfloat16)


def gather_rows(hot, values):
    return jnp.dot(hot, values, preferred_element_type=jnp.float32)


def scatter_rows(hot, values):
    return lax.dot_general(
        hot, values, (((0,), (0,)), ((), ())), preferred_element_type=jnp.float32
    )


AXES = ("lat", "lon")
RINGS = ("x", "y", "z")


def device_of(zh, y, zl, x, core):
    return (zh * 4 + y) * 16 + zl * 8 + x * 2 + core


def all_devices():
    for zh in range(2):
        for y in range(4):
            for zl in range(2):
                for x in range(4):
                    for core in range(2):
                        yield zh, y, zl, x, core


def core_pairs():
    return [(device_of(zh, y, zl, x, c), device_of(zh, y, zl, x, 1 - c)) for zh, y, zl, x, c in all_devices()]


def ring_pairs(ring, shift):
    pairs = []
    for zh, y, zl, x, c in all_devices():
        tx, ty, tz = x, y, zh * 2 + zl
        if ring == "x":
            tx = (x + shift) % 4
        elif ring == "y":
            ty = (y + shift) % 4
        else:
            tz = (tz + shift) % 4
        pairs.append((device_of(zh, y, zl, x, c), device_of(tz // 2, ty, tz % 2, tx, c)))
    return pairs


def ring_positions():
    lat = lax.axis_index("lat")
    lon = lax.axis_index("lon")
    return {"x": (lon // 2) % 4, "y": lat % 4, "z": (lat // 4) * 2 + lon // 8}, lon % 2


def place(stack, own_at):
    gathered = jnp.zeros_like(stack)
    for s in range(stack.shape[0]):
        gathered = lax.dynamic_update_index_in_dim(gathered, stack[s], (own_at - s) % stack.shape[0], 0)
    return gathered


def tiles_of(matrix):
    rows, cols = matrix.shape
    return matrix.reshape(rows // 8, 8, cols // 128, 128).transpose(0, 2, 1, 3).reshape(-1, 128)


def from_tiles(packed, shape):
    rows, cols = shape
    return packed.reshape(rows // 8, cols // 128, 8, 128).transpose(0, 2, 1, 3).reshape(rows, cols)


def tree_allreduce(parts, after):
    lanes = 128
    rows = [p.size // lanes for p in parts]
    data = jnp.concatenate([tiles_of(p) for p in parts], axis=0)
    total = data.shape[0]
    unit = 2 * 64 * 8
    padded = -(-total // unit) * unit
    block = padded // (2 * 64)
    data = jnp.pad(data, ((0, padded - total), (0, 0))).reshape(2, 4, 4, 4, block, lanes)
    pos, core = ring_positions()
    mine = lax.dynamic_index_in_dim(data, core, 0, keepdims=False)
    other = lax.dynamic_index_in_dim(data, 1 - core, 0, keepdims=False)
    chunk = mine + lax.ppermute(other, AXES, core_pairs())
    for ring in RINGS:
        if ring == "y":
            chunk = chunk + after
        p = pos[ring]
        acc = lax.dynamic_index_in_dim(chunk, p, 0, keepdims=False)
        for s in range(1, 4):
            piece = lax.dynamic_index_in_dim(chunk, (p + s) % 4, 0, keepdims=False)
            acc = acc + lax.ppermute(piece, AXES, ring_pairs(ring, s))
        chunk = acc
    chunk = chunk.astype(jnp.bfloat16)
    for ring in reversed(RINGS):
        got = [chunk] + [lax.ppermute(chunk, AXES, ring_pairs(ring, s)) for s in range(1, 4)]
        chunk = place(jnp.stack(got), pos[ring])
    both = place(jnp.stack([chunk, lax.ppermute(chunk, AXES, core_pairs())]), core)
    flat = both.reshape(padded, lanes)[:total].astype(jnp.float32)
    out, at = [], 0
    for p, r in zip(parts, rows):
        out.append(from_tiles(flat[at : at + r], p.shape))
        at += r
    return out


def silu_slope(value):
    sig = jax.nn.sigmoid(value)
    return sig * (1.0 + value * (1.0 - sig))


def dilated(extended, conv_taps, dilation, transpose, rows, cols):
    centre = extended[DMAX : DMAX + rows, DMAX : DMAX + cols].astype(jnp.float32)
    result = conv_taps[0] * centre
    for offset in range(1, DMAX + 1):
        select = (dilation == offset).astype(jnp.float32)
        west = extended[DMAX : DMAX + rows, DMAX - offset : DMAX - offset + cols].astype(
            jnp.float32
        )
        east = extended[DMAX : DMAX + rows, DMAX + offset : DMAX + offset + cols].astype(
            jnp.float32
        )
        south = extended[DMAX - offset : DMAX - offset + rows, DMAX : DMAX + cols].astype(
            jnp.float32
        )
        north = extended[DMAX + offset : DMAX + offset + rows, DMAX : DMAX + cols].astype(
            jnp.float32
        )
        if transpose:
            west, east, south, north = (east, west, north, south)
        result = result + select * (
            conv_taps[1] * west + conv_taps[2] * east + conv_taps[3] * south + conv_taps[4] * north
        )
    return result


def dilated_once(extended, conv_taps, dilation, rows, cols):
    centre = extended[DMAX : DMAX + rows, DMAX : DMAX + cols].astype(jnp.float32)
    sides = []
    for row_at, col_at in ((0, -1), (0, 1), (-1, 0), (1, 0)):
        picked = None
        for offset in range(DMAX, 0, -1):
            r0 = DMAX + row_at * offset
            c0 = DMAX + col_at * offset
            window = extended[r0 : r0 + rows, c0 : c0 + cols].astype(jnp.float32)
            picked = window if picked is None else jnp.where(dilation == offset, window, picked)
        sides.append(picked)
    west, east, south, north = sides
    return conv_taps[0] * centre + (
        conv_taps[1] * west + conv_taps[2] * east + conv_taps[3] * south + conv_taps[4] * north
    )


def polar_rows(extended, rows):
    band_rows = lax.axis_index("lat") * rows + jnp.arange(-DMAX, rows + DMAX)
    inside = (band_rows >= 0) & (band_rows < lax.axis_size("lat") * rows)
    return extended * inside[:, None, None].astype(extended.dtype)


def local(
    atmosphere,
    ocean_state,
    dilation,
    conv_taps,
    atmosphere_gain,
    ocean_gain,
    inner_weight,
    outer_weight,
    flux_weight,
    ocean_inner,
    ocean_outer,
    land_sea,
    send_cell,
    slot_counts,
    slot_area,
    recv_cell,
    atmosphere_cot,
    ocean_cot,
):
    rows, cols, channels = atmosphere.shape
    cells = rows * cols
    lat_count = lax.axis_size("lat")
    lon_count = lax.axis_size("lon")
    devices = lat_count * lon_count
    slots = send_cell.shape[2]
    sea_width = flux_weight.shape[1]
    sea_cells = ocean_state.shape[0]
    air_factor = float(cells * devices) ** (-0.5)
    sea_factor = float(sea_cells * devices) ** (-0.5)
    extended = polar_rows(with_halo(atmosphere, (("lat", 0), ("lon", 1)), DMAX), rows)
    conv_cells = lax.optimization_barrier(
        dilated_once(extended, conv_taps, dilation, rows, cols).reshape(cells, channels)
    )
    scale_air = lax.rsqrt(jnp.mean(conv_cells * conv_cells, axis=-1, keepdims=True) + 1e-06)
    normed = (conv_cells * scale_air * atmosphere_gain).astype(jnp.bfloat16)
    pre = jnp.dot(normed, inner_weight, preferred_element_type=jnp.float32)
    hidden = jax.nn.silu(pre).astype(jnp.bfloat16)
    air_out = (
        conv_cells + jnp.dot(hidden, outer_weight, preferred_element_type=jnp.float32)
    ).astype(jnp.bfloat16)
    sea_mask = land_sea.reshape(cells, 1).astype(jnp.float32)
    flux_rows = (
        sea_mask * jnp.dot(air_out, flux_weight, preferred_element_type=jnp.float32)
    ).astype(jnp.bfloat16)
    live_slots = (jnp.arange(slots)[None, :] < slot_counts[0][:, None]).astype(jnp.float32)
    slot_scale = (slot_area[0] * live_slots)[..., None]
    send_hot = one_hot(send_cell[0], cells)
    recv_hot = one_hot(recv_cell[0], sea_cells)
    picked = gather_rows(send_hot, flux_rows).reshape(devices, slots, sea_width)
    outgoing = (picked * slot_scale).astype(jnp.bfloat16)
    arrived = lax.all_to_all(outgoing, ("lat", "lon"), split_axis=0, concat_axis=0, tiled=True)
    coupled = scatter_rows(recv_hot, arrived.reshape(-1, sea_width))
    sea_in = ocean_state.astype(jnp.float32) + coupled
    scale_sea = lax.rsqrt(jnp.mean(sea_in * sea_in, axis=-1, keepdims=True) + 1e-06)
    sea_normed = (sea_in * scale_sea * ocean_gain).astype(jnp.bfloat16)
    sea_pre = jnp.dot(sea_normed, ocean_inner, preferred_element_type=jnp.float32)
    sea_hidden = jax.nn.silu(sea_pre).astype(jnp.bfloat16)
    sea_vdown = jnp.dot(sea_hidden.T, ocean_cot, preferred_element_type=jnp.float32)
    sea_ghid = jnp.dot(ocean_cot, ocean_outer.T, preferred_element_type=jnp.float32)
    sea_gpre = (sea_ghid * silu_slope(sea_pre)).astype(jnp.bfloat16)
    sea_vup = jnp.dot(sea_normed.T, sea_gpre, preferred_element_type=jnp.float32)
    sea_gnorm = jnp.dot(sea_gpre, ocean_inner.T, preferred_element_type=jnp.float32)
    sea_mean = jnp.mean(sea_in * ocean_gain * sea_gnorm, axis=-1, keepdims=True)
    sea_grad = (
        ocean_cot.astype(jnp.float32)
        + scale_sea * ocean_gain * sea_gnorm
        - sea_in * scale_sea**3 * sea_mean
    )
    grad_ocean = sea_grad.astype(jnp.bfloat16)
    slot_return = (
        gather_rows(recv_hot, grad_ocean).astype(jnp.bfloat16).reshape(devices, slots, sea_width)
    )
    returned = lax.all_to_all(slot_return, ("lat", "lon"), split_axis=0, concat_axis=0, tiled=True)
    addends = (returned.astype(jnp.float32) * slot_scale).reshape(-1, sea_width)
    addends_hi = addends.astype(jnp.bfloat16)
    addends_lo = (addends - addends_hi.astype(jnp.float32)).astype(jnp.bfloat16)
    flux_grad = scatter_rows(send_hot, addends_hi) + scatter_rows(send_hot, addends_lo)
    flux_masked = (sea_mask * flux_grad).astype(jnp.bfloat16)
    flux_wsum = jnp.dot(air_out.T, flux_masked, preferred_element_type=jnp.float32)
    air_grad = atmosphere_cot.reshape(cells, channels).astype(jnp.float32) + jnp.dot(
        flux_masked, flux_weight.T, preferred_element_type=jnp.float32
    )
    air_gradb = air_grad.astype(jnp.bfloat16)
    outer_sum = jnp.dot(hidden.T, air_gradb, preferred_element_type=jnp.float32)
    hid_grad = jnp.dot(air_gradb, outer_weight.T, preferred_element_type=jnp.float32)
    pre_grad = (hid_grad * silu_slope(pre)).astype(jnp.bfloat16)
    inner_sum = jnp.dot(normed.T, pre_grad, preferred_element_type=jnp.float32)
    norm_grad = jnp.dot(pre_grad, inner_weight.T, preferred_element_type=jnp.float32)
    air_mean = jnp.mean(conv_cells * atmosphere_gain * norm_grad, axis=-1, keepdims=True)
    conv_grad = (
        air_grad + scale_air * atmosphere_gain * norm_grad - conv_cells * scale_air**3 * air_mean
    ).astype(jnp.bfloat16)
    grad_extended = polar_rows(
        with_halo(conv_grad.reshape(rows, cols, channels), (("lat", 0), ("lon", 1)), DMAX), rows
    )
    grad_stencil = dilated(grad_extended, conv_taps, dilation, True, rows, cols)
    grad_atmosphere = grad_stencil.astype(jnp.bfloat16)
    summed = tree_allreduce(
        (
            inner_sum * air_factor,
            outer_sum * air_factor,
            flux_wsum * air_factor,
            sea_vup * sea_factor,
            sea_vdown * sea_factor,
        ),
        grad_stencil[0, 0, 0] * 0.0,
    )
    return (grad_atmosphere, grad_ocean) + tuple(summed)


def solution(mesh):
    in_specs = (
        P("lat", "lon", None),
        P(("lat", "lon"), None),
        P(),
        P(),
        P(),
        P(),
        P(),
        P(),
        P(),
        P(),
        P(),
        P("lat", "lon"),
        P(("lat", "lon"), None, None),
        P(("lat", "lon"), None),
        P(("lat", "lon"), None, None),
        P(("lat", "lon"), None, None),
        P("lat", "lon", None),
        P(("lat", "lon"), None),
    )
    out_specs = (P("lat", "lon", None), P(("lat", "lon"), None), P(), P(), P(), P(), P())
    return jax.shard_map(local, mesh=mesh, in_specs=in_specs, out_specs=out_specs, check_vma=False)
```

```python
import jax
import jax.numpy as jnp
from jax import lax
from jax.sharding import PartitionSpec as P

DMAX = 4


def with_halo(block, sides, width):
    (lat_axis, lat_dim), (lon_axis, lon_dim) = sides
    pieces = []
    for axis, dim in sides:
        count = lax.axis_size(axis)
        forward = [(i, i + 1) for i in range(count - 1)]
        forward.append((count - 1, 0))
        backward = [(target, source) for source, target in forward]
        low = lax.ppermute(
            lax.slice_in_dim(block, block.shape[dim] - width, None, axis=dim), axis, forward
        )
        high = lax.ppermute(lax.slice_in_dim(block, 0, width, axis=dim), axis, backward)
        pieces.append((low, high))
    (south, north), (west, east) = pieces
    rows = jnp.concatenate([south, block, north], axis=lat_dim)
    pad = [(0, 0)] * block.ndim
    pad[lat_dim] = (width, width)
    west = jnp.pad(west, pad)
    east = jnp.pad(east, pad)
    return jnp.concatenate([west, rows, east], axis=lon_dim)


def one_hot(index, size):
    return (index.reshape(-1, 1) == jnp.arange(size)[None, :]).astype(jnp.bfloat16)


def gather_rows(hot, values):
    return jnp.dot(hot, values, preferred_element_type=jnp.float32)


def scatter_rows(hot, values):
    return lax.dot_general(
        hot, values, (((0,), (0,)), ((), ())), preferred_element_type=jnp.float32
    )


AXES = ("lat", "lon")
RINGS = ("x", "y", "z")


def device_of(zh, y, zl, x, core):
    return (zh * 4 + y) * 16 + zl * 8 + x * 2 + core


def all_devices():
    for zh in range(2):
        for y in range(4):
            for zl in range(2):
                for x in range(4):
                    for core in range(2):
                        yield zh, y, zl, x, core


def core_pairs():
    return [(device_of(zh, y, zl, x, c), device_of(zh, y, zl, x, 1 - c)) for zh, y, zl, x, c in all_devices()]


def ring_pairs(ring, shift):
    pairs = []
    for zh, y, zl, x, c in all_devices():
        tx, ty, tz = x, y, zh * 2 + zl
        if ring == "x":
            tx = (x + shift) % 4
        elif ring == "y":
            ty = (y + shift) % 4
        else:
            tz = (tz + shift) % 4
        pairs.append((device_of(zh, y, zl, x, c), device_of(tz // 2, ty, tz % 2, tx, c)))
    return pairs


def ring_positions():
    lat = lax.axis_index("lat")
    lon = lax.axis_index("lon")
    return {"x": (lon // 2) % 4, "y": lat % 4, "z": (lat // 4) * 2 + lon // 8}, lon % 2


def place(stack, own_at):
    gathered = jnp.zeros_like(stack)
    for s in range(stack.shape[0]):
        gathered = lax.dynamic_update_index_in_dim(gathered, stack[s], (own_at - s) % stack.shape[0], 0)
    return gathered


def tiles_of(matrix):
    rows, cols = matrix.shape
    return matrix.reshape(rows // 8, 8, cols // 128, 128).transpose(0, 2, 1, 3).reshape(-1, 128)


def from_tiles(packed, shape):
    rows, cols = shape
    return packed.reshape(rows // 8, cols // 128, 8, 128).transpose(0, 2, 1, 3).reshape(rows, cols)


def ring_scatter(chunk, p, ring):
    half = chunk.shape[-2] // 2
    sums = []
    for shift, lo, hi in ((1, 0, half), (-1, half, chunk.shape[-2])):
        own = chunk[..., lo:hi, :]
        acc = lax.dynamic_index_in_dim(own, (p - shift) % 4, 0, keepdims=False)
        for step in range(3):
            got = lax.ppermute(acc, AXES, ring_pairs(ring, shift % 4))
            acc = got + lax.dynamic_index_in_dim(own, (p - shift * (step + 2)) % 4, 0, keepdims=False)
        sums.append(acc)
    return jnp.concatenate(sums, axis=-2)


def tree_allreduce(parts, after):
    lanes = 128
    rows = [p.size // lanes for p in parts]
    data = jnp.concatenate([tiles_of(p) for p in parts], axis=0)
    total = data.shape[0]
    unit = 2 * 64 * 8
    padded = -(-total // unit) * unit
    block = padded // (2 * 64)
    data = jnp.pad(data, ((0, padded - total), (0, 0))).reshape(2, 4, 4, 4, block, lanes)
    pos, core = ring_positions()
    mine = lax.dynamic_index_in_dim(data, core, 0, keepdims=False)
    other = lax.dynamic_index_in_dim(data, 1 - core, 0, keepdims=False)
    chunk = mine + lax.ppermute(other, AXES, core_pairs())
    for ring in RINGS:
        if ring == "y":
            chunk = chunk + after
        p = pos[ring]
        if ring == "x":
            chunk = ring_scatter(chunk, p, ring)
            continue
        acc = lax.dynamic_index_in_dim(chunk, p, 0, keepdims=False)
        for s in range(1, 4):
            piece = lax.dynamic_index_in_dim(chunk, (p + s) % 4, 0, keepdims=False)
            acc = acc + lax.ppermute(piece, AXES, ring_pairs(ring, s))
        chunk = acc
    chunk = chunk.astype(jnp.bfloat16)
    for ring in reversed(RINGS):
        got = [chunk] + [lax.ppermute(chunk, AXES, ring_pairs(ring, s)) for s in range(1, 4)]
        chunk = place(jnp.stack(got), pos[ring])
    both = place(jnp.stack([chunk, lax.ppermute(chunk, AXES, core_pairs())]), core)
    flat = both.reshape(padded, lanes)[:total].astype(jnp.float32)
    out, at = [], 0
    for p, r in zip(parts, rows):
        out.append(from_tiles(flat[at : at + r], p.shape))
        at += r
    return out


def silu_slope(value):
    sig = jax.nn.sigmoid(value)
    return sig * (1.0 + value * (1.0 - sig))


def dilated(extended, conv_taps, dilation, transpose, rows, cols):
    centre = extended[DMAX : DMAX + rows, DMAX : DMAX + cols].astype(jnp.float32)
    result = conv_taps[0] * centre
    for offset in range(1, DMAX + 1):
        select = (dilation == offset).astype(jnp.float32)
        west = extended[DMAX : DMAX + rows, DMAX - offset : DMAX - offset + cols].astype(
            jnp.float32
        )
        east = extended[DMAX : DMAX + rows, DMAX + offset : DMAX + offset + cols].astype(
            jnp.float32
        )
        south = extended[DMAX - offset : DMAX - offset + rows, DMAX : DMAX + cols].astype(
            jnp.float32
        )
        north = extended[DMAX + offset : DMAX + offset + rows, DMAX : DMAX + cols].astype(
            jnp.float32
        )
        if transpose:
            west, east, south, north = (east, west, north, south)
        result = result + select * (
            conv_taps[1] * west + conv_taps[2] * east + conv_taps[3] * south + conv_taps[4] * north
        )
    return result


def dilated_once(extended, conv_taps, dilation, rows, cols):
    centre = extended[DMAX : DMAX + rows, DMAX : DMAX + cols].astype(jnp.float32)
    sides = []
    for row_at, col_at in ((0, -1), (0, 1), (-1, 0), (1, 0)):
        picked = None
        for offset in range(DMAX, 0, -1):
            r0 = DMAX + row_at * offset
            c0 = DMAX + col_at * offset
            window = extended[r0 : r0 + rows, c0 : c0 + cols].astype(jnp.float32)
            picked = window if picked is None else jnp.where(dilation == offset, window, picked)
        sides.append(picked)
    west, east, south, north = sides
    return conv_taps[0] * centre + (
        conv_taps[1] * west + conv_taps[2] * east + conv_taps[3] * south + conv_taps[4] * north
    )


def polar_rows(extended, rows):
    band_rows = lax.axis_index("lat") * rows + jnp.arange(-DMAX, rows + DMAX)
    inside = (band_rows >= 0) & (band_rows < lax.axis_size("lat") * rows)
    return extended * inside[:, None, None].astype(extended.dtype)


def local(
    atmosphere,
    ocean_state,
    dilation,
    conv_taps,
    atmosphere_gain,
    ocean_gain,
    inner_weight,
    outer_weight,
    flux_weight,
    ocean_inner,
    ocean_outer,
    land_sea,
    send_cell,
    slot_counts,
    slot_area,
    recv_cell,
    atmosphere_cot,
    ocean_cot,
):
    rows, cols, channels = atmosphere.shape
    cells = rows * cols
    lat_count = lax.axis_size("lat")
    lon_count = lax.axis_size("lon")
    devices = lat_count * lon_count
    slots = send_cell.shape[2]
    sea_width = flux_weight.shape[1]
    sea_cells = ocean_state.shape[0]
    air_factor = float(cells * devices) ** (-0.5)
    sea_factor = float(sea_cells * devices) ** (-0.5)
    extended = polar_rows(with_halo(atmosphere, (("lat", 0), ("lon", 1)), DMAX), rows)
    conv_cells = lax.optimization_barrier(
        dilated_once(extended, conv_taps, dilation, rows, cols).reshape(cells, channels)
    )
    scale_air = lax.rsqrt(jnp.mean(conv_cells * conv_cells, axis=-1, keepdims=True) + 1e-06)
    normed = (conv_cells * scale_air * atmosphere_gain).astype(jnp.bfloat16)
    pre = jnp.dot(normed, inner_weight, preferred_element_type=jnp.float32)
    hidden = jax.nn.silu(pre).astype(jnp.bfloat16)
    air_out = (
        conv_cells + jnp.dot(hidden, outer_weight, preferred_element_type=jnp.float32)
    ).astype(jnp.bfloat16)
    sea_mask = land_sea.reshape(cells, 1).astype(jnp.float32)
    flux_rows = (
        sea_mask * jnp.dot(air_out, flux_weight, preferred_element_type=jnp.float32)
    ).astype(jnp.bfloat16)
    live_slots = (jnp.arange(slots)[None, :] < slot_counts[0][:, None]).astype(jnp.float32)
    slot_scale = (slot_area[0] * live_slots)[..., None]
    send_hot = one_hot(send_cell[0], cells)
    recv_hot = one_hot(recv_cell[0], sea_cells)
    picked = gather_rows(send_hot, flux_rows).reshape(devices, slots, sea_width)
    outgoing = (picked * slot_scale).astype(jnp.bfloat16)
    arrived = lax.all_to_all(outgoing, ("lat", "lon"), split_axis=0, concat_axis=0, tiled=True)
    coupled = scatter_rows(recv_hot, arrived.reshape(-1, sea_width))
    sea_in = ocean_state.astype(jnp.float32) + coupled
    scale_sea = lax.rsqrt(jnp.mean(sea_in * sea_in, axis=-1, keepdims=True) + 1e-06)
    sea_normed = (sea_in * scale_sea * ocean_gain).astype(jnp.bfloat16)
    sea_pre = jnp.dot(sea_normed, ocean_inner, preferred_element_type=jnp.float32)
    sea_hidden = jax.nn.silu(sea_pre).astype(jnp.bfloat16)
    sea_vdown = jnp.dot(sea_hidden.T, ocean_cot, preferred_element_type=jnp.float32)
    sea_ghid = jnp.dot(ocean_cot, ocean_outer.T, preferred_element_type=jnp.float32)
    sea_gpre = (sea_ghid * silu_slope(sea_pre)).astype(jnp.bfloat16)
    sea_vup = jnp.dot(sea_normed.T, sea_gpre, preferred_element_type=jnp.float32)
    sea_gnorm = jnp.dot(sea_gpre, ocean_inner.T, preferred_element_type=jnp.float32)
    sea_mean = jnp.mean(sea_in * ocean_gain * sea_gnorm, axis=-1, keepdims=True)
    sea_grad = (
        ocean_cot.astype(jnp.float32)
        + scale_sea * ocean_gain * sea_gnorm
        - sea_in * scale_sea**3 * sea_mean
    )
    grad_ocean = sea_grad.astype(jnp.bfloat16)
    slot_return = (
        gather_rows(recv_hot, grad_ocean).astype(jnp.bfloat16).reshape(devices, slots, sea_width)
    )
    returned = lax.all_to_all(slot_return, ("lat", "lon"), split_axis=0, concat_axis=0, tiled=True)
    addends = (returned.astype(jnp.float32) * slot_scale).reshape(-1, sea_width)
    addends_hi = addends.astype(jnp.bfloat16)
    addends_lo = (addends - addends_hi.astype(jnp.float32)).astype(jnp.bfloat16)
    flux_grad = scatter_rows(send_hot, addends_hi) + scatter_rows(send_hot, addends_lo)
    flux_masked = (sea_mask * flux_grad).astype(jnp.bfloat16)
    flux_wsum = jnp.dot(air_out.T, flux_masked, preferred_element_type=jnp.float32)
    air_grad = atmosphere_cot.reshape(cells, channels).astype(jnp.float32) + jnp.dot(
        flux_masked, flux_weight.T, preferred_element_type=jnp.float32
    )
    air_gradb = air_grad.astype(jnp.bfloat16)
    outer_sum = jnp.dot(hidden.T, air_gradb, preferred_element_type=jnp.float32)
    hid_grad = jnp.dot(air_gradb, outer_weight.T, preferred_element_type=jnp.float32)
    pre_grad = (hid_grad * silu_slope(pre)).astype(jnp.bfloat16)
    inner_sum = jnp.dot(normed.T, pre_grad, preferred_element_type=jnp.float32)
    norm_grad = jnp.dot(pre_grad, inner_weight.T, preferred_element_type=jnp.float32)
    air_mean = jnp.mean(conv_cells * atmosphere_gain * norm_grad, axis=-1, keepdims=True)
    conv_grad = (
        air_grad + scale_air * atmosphere_gain * norm_grad - conv_cells * scale_air**3 * air_mean
    ).astype(jnp.bfloat16)
    grad_extended = polar_rows(
        with_halo(conv_grad.reshape(rows, cols, channels), (("lat", 0), ("lon", 1)), DMAX), rows
    )
    grad_stencil = dilated(grad_extended, conv_taps, dilation, True, rows, cols)
    grad_atmosphere = grad_stencil.astype(jnp.bfloat16)
    summed = tree_allreduce(
        (
            inner_sum * air_factor,
            outer_sum * air_factor,
            flux_wsum * air_factor,
            sea_vup * sea_factor,
            sea_vdown * sea_factor,
        ),
        grad_stencil[0, 0, 0] * 0.0,
    )
    return (grad_atmosphere, grad_ocean) + tuple(summed)


def solution(mesh):
    in_specs = (
        P("lat", "lon", None),
        P(("lat", "lon"), None),
        P(),
        P(),
        P(),
        P(),
        P(),
        P(),
        P(),
        P(),
        P(),
        P("lat", "lon"),
        P(("lat", "lon"), None, None),
        P(("lat", "lon"), None),
        P(("lat", "lon"), None, None),
        P(("lat", "lon"), None, None),
        P("lat", "lon", None),
        P(("lat", "lon"), None),
    )
    out_specs = (P("lat", "lon", None), P(("lat", "lon"), None), P(), P(), P(), P(), P())
    return jax.shard_map(local, mesh=mesh, in_specs=in_specs, out_specs=out_specs, check_vma=False)
```

```python
import jax
import jax.numpy as jnp
from jax import lax
from jax.sharding import PartitionSpec as P

DMAX = 4


def with_halo(block, sides, width):
    (lat_axis, lat_dim), (lon_axis, lon_dim) = sides
    pieces = []
    for axis, dim in sides:
        count = lax.axis_size(axis)
        forward = [(i, i + 1) for i in range(count - 1)]
        forward.append((count - 1, 0))
        backward = [(target, source) for source, target in forward]
        low = lax.ppermute(
            lax.slice_in_dim(block, block.shape[dim] - width, None, axis=dim), axis, forward
        )
        high = lax.ppermute(lax.slice_in_dim(block, 0, width, axis=dim), axis, backward)
        pieces.append((low, high))
    (south, north), (west, east) = pieces
    rows = jnp.concatenate([south, block, north], axis=lat_dim)
    pad = [(0, 0)] * block.ndim
    pad[lat_dim] = (width, width)
    west = jnp.pad(west, pad)
    east = jnp.pad(east, pad)
    return jnp.concatenate([west, rows, east], axis=lon_dim)


def one_hot(index, size):
    return (index.reshape(-1, 1) == jnp.arange(size)[None, :]).astype(jnp.bfloat16)


def gather_rows(hot, values):
    return jnp.dot(hot, values, preferred_element_type=jnp.float32)


def scatter_rows(hot, values):
    return lax.dot_general(
        hot, values, (((0,), (0,)), ((), ())), preferred_element_type=jnp.float32
    )


AXES = ("lat", "lon")
RINGS = ("x", "y", "z")


def device_of(zh, y, zl, x, core):
    return (zh * 4 + y) * 16 + zl * 8 + x * 2 + core


def all_devices():
    for zh in range(2):
        for y in range(4):
            for zl in range(2):
                for x in range(4):
                    for core in range(2):
                        yield zh, y, zl, x, core


def core_pairs():
    return [(device_of(zh, y, zl, x, c), device_of(zh, y, zl, x, 1 - c)) for zh, y, zl, x, c in all_devices()]


def ring_pairs(ring, shift):
    pairs = []
    for zh, y, zl, x, c in all_devices():
        tx, ty, tz = x, y, zh * 2 + zl
        if ring == "x":
            tx = (x + shift) % 4
        elif ring == "y":
            ty = (y + shift) % 4
        else:
            tz = (tz + shift) % 4
        pairs.append((device_of(zh, y, zl, x, c), device_of(tz // 2, ty, tz % 2, tx, c)))
    return pairs


def ring_positions():
    lat = lax.axis_index("lat")
    lon = lax.axis_index("lon")
    return {"x": (lon // 2) % 4, "y": lat % 4, "z": (lat // 4) * 2 + lon // 8}, lon % 2


def place(stack, own_at):
    gathered = jnp.zeros_like(stack)
    for s in range(stack.shape[0]):
        gathered = lax.dynamic_update_index_in_dim(gathered, stack[s], (own_at - s) % stack.shape[0], 0)
    return gathered


def tiles_of(matrix):
    rows, cols = matrix.shape
    return matrix.reshape(rows // 8, 8, cols // 128, 128).transpose(0, 2, 1, 3).reshape(-1, 128)


def from_tiles(packed, shape):
    rows, cols = shape
    return packed.reshape(rows // 8, cols // 128, 8, 128).transpose(0, 2, 1, 3).reshape(rows, cols)


def ring_scatter(chunk, p, ring):
    half = chunk.shape[-2] // 2
    sums = []
    for shift, lo, hi in ((1, 0, half), (-1, half, chunk.shape[-2])):
        own = chunk[..., lo:hi, :]
        acc = lax.dynamic_index_in_dim(own, (p - shift) % 4, 0, keepdims=False)
        for step in range(3):
            got = lax.ppermute(acc, AXES, ring_pairs(ring, shift % 4))
            acc = got + lax.dynamic_index_in_dim(own, (p - shift * (step + 2)) % 4, 0, keepdims=False)
        sums.append(acc)
    return jnp.concatenate(sums, axis=-2)


def ring_gather(chunk, p, ring):
    half = chunk.shape[-2] // 2
    halves = []
    for shift, lo, hi in ((1, 0, half), (-1, half, chunk.shape[-2])):
        cur = chunk[..., lo:hi, :]
        got = [cur]
        for step in range(3):
            cur = lax.ppermute(cur, AXES, ring_pairs(ring, shift % 4))
            got.append(cur)
        if shift < 0:
            got = [got[0]] + got[:0:-1]
        halves.append(place(jnp.stack(got), p))
    return jnp.concatenate(halves, axis=-2)


def tree_allreduce(parts, after):
    lanes = 128
    rows = [p.size // lanes for p in parts]
    data = jnp.concatenate([tiles_of(p) for p in parts], axis=0)
    total = data.shape[0]
    unit = 2 * 64 * 8
    padded = -(-total // unit) * unit
    block = padded // (2 * 64)
    data = jnp.pad(data, ((0, padded - total), (0, 0))).reshape(2, 4, 4, 4, block, lanes)
    pos, core = ring_positions()
    mine = lax.dynamic_index_in_dim(data, core, 0, keepdims=False)
    other = lax.dynamic_index_in_dim(data, 1 - core, 0, keepdims=False)
    chunk = mine + lax.ppermute(other, AXES, core_pairs())
    for ring in RINGS:
        if ring == "y":
            chunk = chunk + after
        p = pos[ring]
        if ring == "x":
            chunk = ring_scatter(chunk, p, ring)
            continue
        acc = lax.dynamic_index_in_dim(chunk, p, 0, keepdims=False)
        for s in range(1, 4):
            piece = lax.dynamic_index_in_dim(chunk, (p + s) % 4, 0, keepdims=False)
            acc = acc + lax.ppermute(piece, AXES, ring_pairs(ring, s))
        chunk = acc
    chunk = chunk.astype(jnp.bfloat16)
    for ring in reversed(RINGS):
        if ring == "x":
            chunk = ring_gather(chunk, pos[ring], ring)
            continue
        got = [chunk] + [lax.ppermute(chunk, AXES, ring_pairs(ring, s)) for s in range(1, 4)]
        chunk = place(jnp.stack(got), pos[ring])
    both = place(jnp.stack([chunk, lax.ppermute(chunk, AXES, core_pairs())]), core)
    flat = both.reshape(padded, lanes)[:total].astype(jnp.float32)
    out, at = [], 0
    for p, r in zip(parts, rows):
        out.append(from_tiles(flat[at : at + r], p.shape))
        at += r
    return out


def silu_slope(value):
    sig = jax.nn.sigmoid(value)
    return sig * (1.0 + value * (1.0 - sig))


def dilated(extended, conv_taps, dilation, transpose, rows, cols):
    centre = extended[DMAX : DMAX + rows, DMAX : DMAX + cols].astype(jnp.float32)
    result = conv_taps[0] * centre
    for offset in range(1, DMAX + 1):
        select = (dilation == offset).astype(jnp.float32)
        west = extended[DMAX : DMAX + rows, DMAX - offset : DMAX - offset + cols].astype(
            jnp.float32
        )
        east = extended[DMAX : DMAX + rows, DMAX + offset : DMAX + offset + cols].astype(
            jnp.float32
        )
        south = extended[DMAX - offset : DMAX - offset + rows, DMAX : DMAX + cols].astype(
            jnp.float32
        )
        north = extended[DMAX + offset : DMAX + offset + rows, DMAX : DMAX + cols].astype(
            jnp.float32
        )
        if transpose:
            west, east, south, north = (east, west, north, south)
        result = result + select * (
            conv_taps[1] * west + conv_taps[2] * east + conv_taps[3] * south + conv_taps[4] * north
        )
    return result


def dilated_once(extended, conv_taps, dilation, rows, cols):
    centre = extended[DMAX : DMAX + rows, DMAX : DMAX + cols].astype(jnp.float32)
    sides = []
    for row_at, col_at in ((0, -1), (0, 1), (-1, 0), (1, 0)):
        picked = None
        for offset in range(DMAX, 0, -1):
            r0 = DMAX + row_at * offset
            c0 = DMAX + col_at * offset
            window = extended[r0 : r0 + rows, c0 : c0 + cols].astype(jnp.float32)
            picked = window if picked is None else jnp.where(dilation == offset, window, picked)
        sides.append(picked)
    west, east, south, north = sides
    return conv_taps[0] * centre + (
        conv_taps[1] * west + conv_taps[2] * east + conv_taps[3] * south + conv_taps[4] * north
    )


def polar_rows(extended, rows):
    band_rows = lax.axis_index("lat") * rows + jnp.arange(-DMAX, rows + DMAX)
    inside = (band_rows >= 0) & (band_rows < lax.axis_size("lat") * rows)
    return extended * inside[:, None, None].astype(extended.dtype)


def local(
    atmosphere,
    ocean_state,
    dilation,
    conv_taps,
    atmosphere_gain,
    ocean_gain,
    inner_weight,
    outer_weight,
    flux_weight,
    ocean_inner,
    ocean_outer,
    land_sea,
    send_cell,
    slot_counts,
    slot_area,
    recv_cell,
    atmosphere_cot,
    ocean_cot,
):
    rows, cols, channels = atmosphere.shape
    cells = rows * cols
    lat_count = lax.axis_size("lat")
    lon_count = lax.axis_size("lon")
    devices = lat_count * lon_count
    slots = send_cell.shape[2]
    sea_width = flux_weight.shape[1]
    sea_cells = ocean_state.shape[0]
    air_factor = float(cells * devices) ** (-0.5)
    sea_factor = float(sea_cells * devices) ** (-0.5)
    extended = polar_rows(with_halo(atmosphere, (("lat", 0), ("lon", 1)), DMAX), rows)
    conv_cells = lax.optimization_barrier(
        dilated_once(extended, conv_taps, dilation, rows, cols).reshape(cells, channels)
    )
    scale_air = lax.rsqrt(jnp.mean(conv_cells * conv_cells, axis=-1, keepdims=True) + 1e-06)
    normed = (conv_cells * scale_air * atmosphere_gain).astype(jnp.bfloat16)
    pre = jnp.dot(normed, inner_weight, preferred_element_type=jnp.float32)
    hidden = jax.nn.silu(pre).astype(jnp.bfloat16)
    air_out = (
        conv_cells + jnp.dot(hidden, outer_weight, preferred_element_type=jnp.float32)
    ).astype(jnp.bfloat16)
    sea_mask = land_sea.reshape(cells, 1).astype(jnp.float32)
    flux_rows = (
        sea_mask * jnp.dot(air_out, flux_weight, preferred_element_type=jnp.float32)
    ).astype(jnp.bfloat16)
    live_slots = (jnp.arange(slots)[None, :] < slot_counts[0][:, None]).astype(jnp.float32)
    slot_scale = (slot_area[0] * live_slots)[..., None]
    send_hot = one_hot(send_cell[0], cells)
    recv_hot = one_hot(recv_cell[0], sea_cells)
    picked = gather_rows(send_hot, flux_rows).reshape(devices, slots, sea_width)
    outgoing = (picked * slot_scale).astype(jnp.bfloat16)
    arrived = lax.all_to_all(outgoing, ("lat", "lon"), split_axis=0, concat_axis=0, tiled=True)
    coupled = scatter_rows(recv_hot, arrived.reshape(-1, sea_width))
    sea_in = ocean_state.astype(jnp.float32) + coupled
    scale_sea = lax.rsqrt(jnp.mean(sea_in * sea_in, axis=-1, keepdims=True) + 1e-06)
    sea_normed = (sea_in * scale_sea * ocean_gain).astype(jnp.bfloat16)
    sea_pre = jnp.dot(sea_normed, ocean_inner, preferred_element_type=jnp.float32)
    sea_hidden = jax.nn.silu(sea_pre).astype(jnp.bfloat16)
    sea_vdown = jnp.dot(sea_hidden.T, ocean_cot, preferred_element_type=jnp.float32)
    sea_ghid = jnp.dot(ocean_cot, ocean_outer.T, preferred_element_type=jnp.float32)
    sea_gpre = (sea_ghid * silu_slope(sea_pre)).astype(jnp.bfloat16)
    sea_vup = jnp.dot(sea_normed.T, sea_gpre, preferred_element_type=jnp.float32)
    sea_gnorm = jnp.dot(sea_gpre, ocean_inner.T, preferred_element_type=jnp.float32)
    sea_mean = jnp.mean(sea_in * ocean_gain * sea_gnorm, axis=-1, keepdims=True)
    sea_grad = (
        ocean_cot.astype(jnp.float32)
        + scale_sea * ocean_gain * sea_gnorm
        - sea_in * scale_sea**3 * sea_mean
    )
    grad_ocean = sea_grad.astype(jnp.bfloat16)
    slot_return = (
        gather_rows(recv_hot, grad_ocean).astype(jnp.bfloat16).reshape(devices, slots, sea_width)
    )
    returned = lax.all_to_all(slot_return, ("lat", "lon"), split_axis=0, concat_axis=0, tiled=True)
    addends = (returned.astype(jnp.float32) * slot_scale).reshape(-1, sea_width)
    addends_hi = addends.astype(jnp.bfloat16)
    addends_lo = (addends - addends_hi.astype(jnp.float32)).astype(jnp.bfloat16)
    flux_grad = scatter_rows(send_hot, addends_hi) + scatter_rows(send_hot, addends_lo)
    flux_masked = (sea_mask * flux_grad).astype(jnp.bfloat16)
    flux_wsum = jnp.dot(air_out.T, flux_masked, preferred_element_type=jnp.float32)
    air_grad = atmosphere_cot.reshape(cells, channels).astype(jnp.float32) + jnp.dot(
        flux_masked, flux_weight.T, preferred_element_type=jnp.float32
    )
    air_gradb = air_grad.astype(jnp.bfloat16)
    outer_sum = jnp.dot(hidden.T, air_gradb, preferred_element_type=jnp.float32)
    hid_grad = jnp.dot(air_gradb, outer_weight.T, preferred_element_type=jnp.float32)
    pre_grad = (hid_grad * silu_slope(pre)).astype(jnp.bfloat16)
    inner_sum = jnp.dot(normed.T, pre_grad, preferred_element_type=jnp.float32)
    norm_grad = jnp.dot(pre_grad, inner_weight.T, preferred_element_type=jnp.float32)
    air_mean = jnp.mean(conv_cells * atmosphere_gain * norm_grad, axis=-1, keepdims=True)
    conv_grad = (
        air_grad + scale_air * atmosphere_gain * norm_grad - conv_cells * scale_air**3 * air_mean
    ).astype(jnp.bfloat16)
    grad_extended = polar_rows(
        with_halo(conv_grad.reshape(rows, cols, channels), (("lat", 0), ("lon", 1)), DMAX), rows
    )
    grad_stencil = dilated(grad_extended, conv_taps, dilation, True, rows, cols)
    grad_atmosphere = grad_stencil.astype(jnp.bfloat16)
    summed = tree_allreduce(
        (
            inner_sum * air_factor,
            outer_sum * air_factor,
            flux_wsum * air_factor,
            sea_vup * sea_factor,
            sea_vdown * sea_factor,
        ),
        grad_stencil[0, 0, 0] * 0.0,
    )
    return (grad_atmosphere, grad_ocean) + tuple(summed)


def solution(mesh):
    in_specs = (
        P("lat", "lon", None),
        P(("lat", "lon"), None),
        P(),
        P(),
        P(),
        P(),
        P(),
        P(),
        P(),
        P(),
        P(),
        P("lat", "lon"),
        P(("lat", "lon"), None, None),
        P(("lat", "lon"), None),
        P(("lat", "lon"), None, None),
        P(("lat", "lon"), None, None),
        P("lat", "lon", None),
        P(("lat", "lon"), None),
    )
    out_specs = (P("lat", "lon", None), P(("lat", "lon"), None), P(), P(), P(), P(), P())
    return jax.shard_map(local, mesh=mesh, in_specs=in_specs, out_specs=out_specs, check_vma=False)
```

```python
import jax
import jax.numpy as jnp
from jax import lax
from jax.sharding import PartitionSpec as P

DMAX = 4


def with_halo(block, sides, width):
    (lat_axis, lat_dim), (lon_axis, lon_dim) = sides
    pieces = []
    for axis, dim in sides:
        count = lax.axis_size(axis)
        forward = [(i, i + 1) for i in range(count - 1)]
        forward.append((count - 1, 0))
        backward = [(target, source) for source, target in forward]
        low = lax.ppermute(
            lax.slice_in_dim(block, block.shape[dim] - width, None, axis=dim), axis, forward
        )
        high = lax.ppermute(lax.slice_in_dim(block, 0, width, axis=dim), axis, backward)
        pieces.append((low, high))
    (south, north), (west, east) = pieces
    rows = jnp.concatenate([south, block, north], axis=lat_dim)
    pad = [(0, 0)] * block.ndim
    pad[lat_dim] = (width, width)
    west = jnp.pad(west, pad)
    east = jnp.pad(east, pad)
    return jnp.concatenate([west, rows, east], axis=lon_dim)


def one_hot(index, size):
    return (index.reshape(-1, 1) == jnp.arange(size)[None, :]).astype(jnp.bfloat16)


def gather_rows(hot, values):
    return jnp.dot(hot, values, preferred_element_type=jnp.float32)


def scatter_rows(hot, values):
    return lax.dot_general(
        hot, values, (((0,), (0,)), ((), ())), preferred_element_type=jnp.float32
    )


AXES = ("lat", "lon")
RINGS = ("x", "y", "z")


def device_of(zh, y, zl, x, core):
    return (zh * 4 + y) * 16 + zl * 8 + x * 2 + core


def all_devices():
    for zh in range(2):
        for y in range(4):
            for zl in range(2):
                for x in range(4):
                    for core in range(2):
                        yield zh, y, zl, x, core


def core_pairs():
    return [(device_of(zh, y, zl, x, c), device_of(zh, y, zl, x, 1 - c)) for zh, y, zl, x, c in all_devices()]


def ring_pairs(ring, shift):
    pairs = []
    for zh, y, zl, x, c in all_devices():
        tx, ty, tz = x, y, zh * 2 + zl
        if ring == "x":
            tx = (x + shift) % 4
        elif ring == "y":
            ty = (y + shift) % 4
        else:
            tz = (tz + shift) % 4
        pairs.append((device_of(zh, y, zl, x, c), device_of(tz // 2, ty, tz % 2, tx, c)))
    return pairs


def ring_positions():
    lat = lax.axis_index("lat")
    lon = lax.axis_index("lon")
    return {"x": (lon // 2) % 4, "y": lat % 4, "z": (lat // 4) * 2 + lon // 8}, lon % 2


def place(stack, own_at):
    gathered = jnp.zeros_like(stack)
    for s in range(stack.shape[0]):
        gathered = lax.dynamic_update_index_in_dim(gathered, stack[s], (own_at - s) % stack.shape[0], 0)
    return gathered


def tiles_of(matrix):
    rows, cols = matrix.shape
    return matrix.reshape(rows // 8, 8, cols // 128, 128).transpose(0, 2, 1, 3).reshape(-1, 128)


def from_tiles(packed, shape):
    rows, cols = shape
    return packed.reshape(rows // 8, cols // 128, 8, 128).transpose(0, 2, 1, 3).reshape(rows, cols)


def ring_scatter(chunk, p, ring):
    half = chunk.shape[-2] // 2
    sums = []
    for shift, lo, hi in ((1, 0, half), (-1, half, chunk.shape[-2])):
        own = chunk[..., lo:hi, :]
        acc = lax.dynamic_index_in_dim(own, (p - shift) % 4, 0, keepdims=False)
        for step in range(3):
            got = lax.ppermute(acc, AXES, ring_pairs(ring, shift % 4))
            acc = got + lax.dynamic_index_in_dim(own, (p - shift * (step + 2)) % 4, 0, keepdims=False)
        sums.append(acc)
    return jnp.concatenate(sums, axis=-2)


def tree_allreduce(parts, after):
    lanes = 128
    rows = [p.size // lanes for p in parts]
    data = jnp.concatenate([tiles_of(p) for p in parts], axis=0)
    total = data.shape[0]
    unit = 2 * 64 * 8
    padded = -(-total // unit) * unit
    block = padded // (2 * 64)
    data = jnp.pad(data, ((0, padded - total), (0, 0))).reshape(2, 4, 4, 4, block, lanes)
    pos, core = ring_positions()
    mine = lax.dynamic_index_in_dim(data, core, 0, keepdims=False)
    other = lax.dynamic_index_in_dim(data, 1 - core, 0, keepdims=False)
    chunk = mine + lax.ppermute(other, AXES, core_pairs())
    for ring in RINGS:
        if ring == "z":
            chunk = chunk + after
        p = pos[ring]
        if ring == "x":
            chunk = ring_scatter(chunk, p, ring)
            continue
        acc = lax.dynamic_index_in_dim(chunk, p, 0, keepdims=False)
        for s in range(1, 4):
            piece = lax.dynamic_index_in_dim(chunk, (p + s) % 4, 0, keepdims=False)
            acc = acc + lax.ppermute(piece, AXES, ring_pairs(ring, s))
        chunk = acc
    chunk = chunk.astype(jnp.bfloat16)
    for ring in reversed(RINGS):
        got = [chunk] + [lax.ppermute(chunk, AXES, ring_pairs(ring, s)) for s in range(1, 4)]
        chunk = place(jnp.stack(got), pos[ring])
    both = place(jnp.stack([chunk, lax.ppermute(chunk, AXES, core_pairs())]), core)
    flat = both.reshape(padded, lanes)[:total].astype(jnp.float32)
    out, at = [], 0
    for p, r in zip(parts, rows):
        out.append(from_tiles(flat[at : at + r], p.shape))
        at += r
    return out


def silu_slope(value):
    sig = jax.nn.sigmoid(value)
    return sig * (1.0 + value * (1.0 - sig))


def dilated(extended, conv_taps, dilation, transpose, rows, cols):
    centre = extended[DMAX : DMAX + rows, DMAX : DMAX + cols].astype(jnp.float32)
    result = conv_taps[0] * centre
    for offset in range(1, DMAX + 1):
        select = (dilation == offset).astype(jnp.float32)
        west = extended[DMAX : DMAX + rows, DMAX - offset : DMAX - offset + cols].astype(
            jnp.float32
        )
        east = extended[DMAX : DMAX + rows, DMAX + offset : DMAX + offset + cols].astype(
            jnp.float32
        )
        south = extended[DMAX - offset : DMAX - offset + rows, DMAX : DMAX + cols].astype(
            jnp.float32
        )
        north = extended[DMAX + offset : DMAX + offset + rows, DMAX : DMAX + cols].astype(
            jnp.float32
        )
        if transpose:
            west, east, south, north = (east, west, north, south)
        result = result + select * (
            conv_taps[1] * west + conv_taps[2] * east + conv_taps[3] * south + conv_taps[4] * north
        )
    return result


def dilated_once(extended, conv_taps, dilation, rows, cols):
    centre = extended[DMAX : DMAX + rows, DMAX : DMAX + cols].astype(jnp.float32)
    sides = []
    for row_at, col_at in ((0, -1), (0, 1), (-1, 0), (1, 0)):
        picked = None
        for offset in range(DMAX, 0, -1):
            r0 = DMAX + row_at * offset
            c0 = DMAX + col_at * offset
            window = extended[r0 : r0 + rows, c0 : c0 + cols].astype(jnp.float32)
            picked = window if picked is None else jnp.where(dilation == offset, window, picked)
        sides.append(picked)
    west, east, south, north = sides
    return conv_taps[0] * centre + (
        conv_taps[1] * west + conv_taps[2] * east + conv_taps[3] * south + conv_taps[4] * north
    )


def polar_rows(extended, rows):
    band_rows = lax.axis_index("lat") * rows + jnp.arange(-DMAX, rows + DMAX)
    inside = (band_rows >= 0) & (band_rows < lax.axis_size("lat") * rows)
    return extended * inside[:, None, None].astype(extended.dtype)


def local(
    atmosphere,
    ocean_state,
    dilation,
    conv_taps,
    atmosphere_gain,
    ocean_gain,
    inner_weight,
    outer_weight,
    flux_weight,
    ocean_inner,
    ocean_outer,
    land_sea,
    send_cell,
    slot_counts,
    slot_area,
    recv_cell,
    atmosphere_cot,
    ocean_cot,
):
    rows, cols, channels = atmosphere.shape
    cells = rows * cols
    lat_count = lax.axis_size("lat")
    lon_count = lax.axis_size("lon")
    devices = lat_count * lon_count
    slots = send_cell.shape[2]
    sea_width = flux_weight.shape[1]
    sea_cells = ocean_state.shape[0]
    air_factor = float(cells * devices) ** (-0.5)
    sea_factor = float(sea_cells * devices) ** (-0.5)
    extended = polar_rows(with_halo(atmosphere, (("lat", 0), ("lon", 1)), DMAX), rows)
    conv_cells = lax.optimization_barrier(
        dilated_once(extended, conv_taps, dilation, rows, cols).reshape(cells, channels)
    )
    scale_air = lax.rsqrt(jnp.mean(conv_cells * conv_cells, axis=-1, keepdims=True) + 1e-06)
    normed = (conv_cells * scale_air * atmosphere_gain).astype(jnp.bfloat16)
    pre = jnp.dot(normed, inner_weight, preferred_element_type=jnp.float32)
    hidden = jax.nn.silu(pre).astype(jnp.bfloat16)
    air_out = (
        conv_cells + jnp.dot(hidden, outer_weight, preferred_element_type=jnp.float32)
    ).astype(jnp.bfloat16)
    sea_mask = land_sea.reshape(cells, 1).astype(jnp.float32)
    flux_rows = (
        sea_mask * jnp.dot(air_out, flux_weight, preferred_element_type=jnp.float32)
    ).astype(jnp.bfloat16)
    live_slots = (jnp.arange(slots)[None, :] < slot_counts[0][:, None]).astype(jnp.float32)
    slot_scale = (slot_area[0] * live_slots)[..., None]
    send_hot = one_hot(send_cell[0], cells)
    recv_hot = one_hot(recv_cell[0], sea_cells)
    picked = gather_rows(send_hot, flux_rows).reshape(devices, slots, sea_width)
    outgoing = (picked * slot_scale).astype(jnp.bfloat16)
    arrived = lax.all_to_all(outgoing, ("lat", "lon"), split_axis=0, concat_axis=0, tiled=True)
    coupled = scatter_rows(recv_hot, arrived.reshape(-1, sea_width))
    sea_in = ocean_state.astype(jnp.float32) + coupled
    scale_sea = lax.rsqrt(jnp.mean(sea_in * sea_in, axis=-1, keepdims=True) + 1e-06)
    sea_normed = (sea_in * scale_sea * ocean_gain).astype(jnp.bfloat16)
    sea_pre = jnp.dot(sea_normed, ocean_inner, preferred_element_type=jnp.float32)
    sea_hidden = jax.nn.silu(sea_pre).astype(jnp.bfloat16)
    sea_vdown = jnp.dot(sea_hidden.T, ocean_cot, preferred_element_type=jnp.float32)
    sea_ghid = jnp.dot(ocean_cot, ocean_outer.T, preferred_element_type=jnp.float32)
    sea_gpre = (sea_ghid * silu_slope(sea_pre)).astype(jnp.bfloat16)
    sea_vup = jnp.dot(sea_normed.T, sea_gpre, preferred_element_type=jnp.float32)
    sea_gnorm = jnp.dot(sea_gpre, ocean_inner.T, preferred_element_type=jnp.float32)
    sea_mean = jnp.mean(sea_in * ocean_gain * sea_gnorm, axis=-1, keepdims=True)
    sea_grad = (
        ocean_cot.astype(jnp.float32)
        + scale_sea * ocean_gain * sea_gnorm
        - sea_in * scale_sea**3 * sea_mean
    )
    grad_ocean = sea_grad.astype(jnp.bfloat16)
    slot_return = (
        gather_rows(recv_hot, grad_ocean).astype(jnp.bfloat16).reshape(devices, slots, sea_width)
    )
    returned = lax.all_to_all(slot_return, ("lat", "lon"), split_axis=0, concat_axis=0, tiled=True)
    addends = (returned.astype(jnp.float32) * slot_scale).reshape(-1, sea_width)
    addends_hi = addends.astype(jnp.bfloat16)
    addends_lo = (addends - addends_hi.astype(jnp.float32)).astype(jnp.bfloat16)
    flux_grad = scatter_rows(send_hot, addends_hi) + scatter_rows(send_hot, addends_lo)
    flux_masked = (sea_mask * flux_grad).astype(jnp.bfloat16)
    flux_wsum = jnp.dot(air_out.T, flux_masked, preferred_element_type=jnp.float32)
    air_grad = atmosphere_cot.reshape(cells, channels).astype(jnp.float32) + jnp.dot(
        flux_masked, flux_weight.T, preferred_element_type=jnp.float32
    )
    air_gradb = air_grad.astype(jnp.bfloat16)
    outer_sum = jnp.dot(hidden.T, air_gradb, preferred_element_type=jnp.float32)
    hid_grad = jnp.dot(air_gradb, outer_weight.T, preferred_element_type=jnp.float32)
    pre_grad = (hid_grad * silu_slope(pre)).astype(jnp.bfloat16)
    inner_sum = jnp.dot(normed.T, pre_grad, preferred_element_type=jnp.float32)
    norm_grad = jnp.dot(pre_grad, inner_weight.T, preferred_element_type=jnp.float32)
    air_mean = jnp.mean(conv_cells * atmosphere_gain * norm_grad, axis=-1, keepdims=True)
    conv_grad = (
        air_grad + scale_air * atmosphere_gain * norm_grad - conv_cells * scale_air**3 * air_mean
    ).astype(jnp.bfloat16)
    grad_extended = polar_rows(
        with_halo(conv_grad.reshape(rows, cols, channels), (("lat", 0), ("lon", 1)), DMAX), rows
    )
    grad_stencil = dilated(grad_extended, conv_taps, dilation, True, rows, cols)
    grad_atmosphere = grad_stencil.astype(jnp.bfloat16)
    summed = tree_allreduce(
        (
            inner_sum * air_factor,
            outer_sum * air_factor,
            flux_wsum * air_factor,
            sea_vup * sea_factor,
            sea_vdown * sea_factor,
        ),
        grad_stencil[0, 0, 0] * 0.0,
    )
    return (grad_atmosphere, grad_ocean) + tuple(summed)


def solution(mesh):
    in_specs = (
        P("lat", "lon", None),
        P(("lat", "lon"), None),
        P(),
        P(),
        P(),
        P(),
        P(),
        P(),
        P(),
        P(),
        P(),
        P("lat", "lon"),
        P(("lat", "lon"), None, None),
        P(("lat", "lon"), None),
        P(("lat", "lon"), None, None),
        P(("lat", "lon"), None, None),
        P("lat", "lon", None),
        P(("lat", "lon"), None),
    )
    out_specs = (P("lat", "lon", None), P(("lat", "lon"), None), P(), P(), P(), P(), P())
    return jax.shard_map(local, mesh=mesh, in_specs=in_specs, out_specs=out_specs, check_vma=False)
```
